32 devices in a mesh: img: 4 (over z), ref: 8 (over y, x, core).
Axes of the slice: x: 2, y: 2, z: 4, core: 2. Of those that a mesh axis runs over, the one named last changes fastest.
Arguments:
- images: bfloat16 [2048, 9216], P(('img', 'ref')), may hold values from -96 to 96
- references: bfloat16 [6912, 9216], P('ref'), may hold values from -0.5 to 0.5
- class_prior: float32 [192], P('ref'), may hold values from 0.2 to 5
Outputs:
- class_sums: float32 [192, 9216], P('ref', 'img')
- class_weights: float32 [192], P('ref')
The draws below stay inside these ranges and needn't reach their ends.
All inputs are finite; a program needn't handle non-finite values.
Results may differ from the reference program's by a relative error of at most 0.0021.
Values may be sent and summed in bfloat16 or wider, within the bound.
No kernel may reach another device: no remote copies, remote signals or barrier semaphores. Data moves between devices by JAX's collectives and lax.ppermute only.
A program may use at most 128 MiB of HBM per device.

```python
import math
import jax
import jax.numpy as jnp
from jax import lax

RAD = 64
ANG = 144
ROT = 36
K = 192
IMG_DEV = 64
NIMG = 2048
N_REF = 8


def class_library(key):
    inner = jax.random.fold_in(key, 11)
    first_key, second_key = jax.random.split(inner)
    ranks = jnp.arange(K).astype(jnp.float32)
    scales = 3.0 ** (ranks / (K - 1)) * jnp.exp(jax.random.uniform(first_key, (K,), jnp.float32, jnp.log(0.5), 0.0))
    templates = jax.random.normal(second_key, (K, RAD, ANG), jnp.float32) * scales[:, None, None] / jnp.sqrt(1.0 * RAD * ANG)
    return templates


def draw_references(key, part):
    templates = class_library(key)
    turned = jnp.stack([jnp.roll(templates, turn_index * (ANG // ROT), axis=2) for turn_index in range(ROT)], axis=1)
    return turned.reshape(K * ROT, RAD * ANG).astype(jnp.bfloat16)


def draw_images(key, part):
    inner = jax.random.fold_in(key, 21)
    keys = jax.random.split(inner, 2)
    rows = jnp.arange(NIMG).astype(jnp.float32)
    rising = 1.0 + 2.0 * rows / (NIMG - 1)
    jitter = jnp.exp(jax.random.uniform(keys[0], (NIMG,), jnp.float32, jnp.log(0.7), jnp.log(1.4)))
    noise = jax.random.normal(keys[1], (NIMG, RAD * ANG), jnp.float32)
    images = noise * (rising * jitter)[:, None]
    return images.astype(jnp.bfloat16)


def level_of(stream_key, shape, cuts, low, largest):
    def one(dim, blocks):
        draws = jax.random.uniform(jax.random.fold_in(jax.random.fold_in(stream_key, 6), dim), (blocks,), jnp.float32, low / len(cuts), largest / len(cuts))
        return jnp.repeat(jnp.exp(draws), shape[dim] // blocks).reshape((-1,) + (1,) * (len(shape) - dim - 1))

    level = one(*cuts[0])
    for cut in cuts[1:]:
        level = level * one(*cut)
    return level


def setup_inputs(seed: int = 0) -> dict:
    key_of = jax.random.split(jax.random.key(seed), 4)
    return {
        "images": draw_images(jax.random.fold_in(key_of[3], 71), 0),
        "references": draw_references(jax.random.fold_in(key_of[3], 71), 0),
        "class_prior": jnp.clip(jnp.exp(math.log(5.0) - 3.218876 * jax.random.uniform(key_of[2], (K,), jnp.float32) ** level_of(key_of[2], (K,), ((0, 8),), -0.2, 0.2)), 0.2, 5.0),
    }


def reference(images, references, class_prior):
    shift_size = ANG // ROT
    grouped = references.reshape(K, ROT, RAD * ANG)
    half_norm = lax.map(lambda block: 0.5 * jnp.sum(jnp.square(block.astype(jnp.float32)), axis=-1), grouped).reshape(K * ROT)
    offsets = jnp.repeat(jnp.log(class_prior), ROT) - half_norm
    group_rows = IMG_DEV * N_REF
    blocks = images.reshape(NIMG // group_rows, group_rows, RAD * ANG)

    def absorb(running, block):
        sums, weight_sum = running
        scores = jnp.dot(block, references.T, preferred_element_type=jnp.float32) + offsets
        top_score = jnp.max(scores, axis=1, keepdims=True)
        raised = jnp.exp(scores - top_score)
        weights = (raised / jnp.sum(raised, axis=1, keepdims=True)).astype(jnp.bfloat16)
        weight_sum = weight_sum + jnp.sum(weights.astype(jnp.float32), axis=0).reshape(K, ROT).sum(axis=1)
        shaped = weights.reshape(-1, K, ROT)
        cycles = block.reshape(-1, RAD, ANG)
        for turn_index in range(ROT):
            turned = jnp.roll(cycles, -turn_index * shift_size, axis=2).reshape(-1, RAD * ANG)
            sums = sums + jnp.dot(shaped[:, :, turn_index].T, turned, preferred_element_type=jnp.float32)
        return (sums, weight_sum), None

    start_state = (jnp.zeros((K, RAD * ANG), jnp.float32), jnp.zeros((K,), jnp.float32))
    (sums, weight_sum), unused = lax.scan(absorb, start_state, blocks)
    return sums, weight_sum
```

```python
import functools

import jax
import jax.numpy as jnp
from jax import lax
from jax.experimental import pallas as pl
from jax.experimental.pallas import tpu as pltpu
from jax.sharding import PartitionSpec as P

ANG = 144
LANES = 128


def pixel_dims(pixels, rotations):
    shift = ANG // rotations
    cycles = pixels // ANG
    per_lane_block = LANES // shift
    halves = cycles // per_lane_block
    return shift, per_lane_block, halves


def to_turn_layout(x, rotations):
    rows, pixels = x.shape
    shift, per_lane_block, halves = pixel_dims(pixels, rotations)
    x = x.reshape(rows, halves, per_lane_block, rotations, shift)
    return x.transpose(0, 1, 3, 2, 4).reshape(rows, pixels)


def from_turn_layout(x, rotations):
    rows, pixels = x.shape
    shift, per_lane_block, halves = pixel_dims(pixels, rotations)
    x = x.reshape(rows, halves, rotations, per_lane_block, shift)
    return x.transpose(0, 1, 3, 2, 4).reshape(rows, pixels)


def turn_sum_kernel(classes_here, rotations, by_turn_ref, images_ref, out_ref, products_ref):
    products_ref[...] = jnp.dot(
        by_turn_ref[...], images_ref[...], preferred_element_type=jnp.float32
    )
    for b in range(rotations):
        total = None
        for turn_index in range(rotations):
            col = ((b + turn_index) % rotations) * LANES
            part = products_ref[
                turn_index * classes_here : (turn_index + 1) * classes_here, col : col + LANES
            ]
            total = part if total is None else total + part
        out_ref[:, b * LANES : (b + 1) * LANES] = total


def turn_and_sum(by_turn, gathered, classes_here, rotations, halves):
    local_refs, n = by_turn.shape
    pixels = gathered.shape[1]
    slab = pixels // halves
    return pl.pallas_call(
        functools.partial(turn_sum_kernel, classes_here, rotations),
        grid=(halves,),
        in_specs=[
            pl.BlockSpec((local_refs, n), lambda h: (0, 0)),
            pl.BlockSpec((n, slab), lambda h: (0, h)),
        ],
        out_specs=pl.BlockSpec((classes_here, slab), lambda h: (0, h)),
        out_shape=jax.ShapeDtypeStruct((classes_here, pixels), jnp.float32),
        scratch_shapes=[pltpu.VMEM((local_refs, slab), jnp.float32)],
        compiler_params=pltpu.CompilerParams(vmem_limit_bytes=60 * 1024 * 1024),
        cost_estimate=pl.CostEstimate(
            flops=2 * local_refs * n * pixels,
            bytes_accessed=2 * local_refs * n + 2 * n * pixels + 4 * classes_here * pixels,
            transcendentals=0,
        ),
    )(by_turn, gathered)


def per_device(images, references, class_prior):
    local_refs, pixels = references.shape
    classes_here = class_prior.shape[0]
    rotations = local_refs // classes_here
    shift, per_lane_block, halves = pixel_dims(pixels, rotations)

    half_norm = 0.5 * jnp.einsum(
        "jp,jp->j", references, references, preferred_element_type=jnp.float32
    )
    offsets = (jnp.log(class_prior)[:, None] - half_norm.reshape(classes_here, rotations)).reshape(
        local_refs
    )
    turned_images = to_turn_layout(images, rotations)
    gathered = lax.all_gather(turned_images, "ref", axis=0, tiled=True)
    turned_refs = to_turn_layout(references, rotations)
    products = lax.dot_general(
        gathered, turned_refs, (((1,), (1,)), ((), ())), preferred_element_type=jnp.float32
    )
    scores = products + offsets
    local_max = jnp.max(scores, axis=1)
    local_sum = jnp.sum(jnp.exp(scores - local_max[:, None]), axis=1)
    stats = lax.all_gather(jnp.stack([local_max, local_sum]), "ref", axis=0)
    top_score = jnp.max(stats[:, 0], axis=0)
    denominator = jnp.sum(stats[:, 1] * jnp.exp(stats[:, 0] - top_score[None, :]), axis=0)
    weights = (jnp.exp(scores - top_score[:, None]) / denominator[:, None]).astype(jnp.bfloat16)
    local_mass = (
        jnp.sum(weights.astype(jnp.float32), axis=0).reshape(classes_here, rotations).sum(axis=1)
    )
    class_weights = lax.psum(local_mass, "img")

    n = weights.shape[0]
    by_turn = weights.reshape(n, classes_here, rotations).transpose(2, 1, 0).reshape(local_refs, n)
    turned_sums = turn_and_sum(by_turn, gathered, classes_here, rotations, halves)
    local_sums = from_turn_layout(turned_sums, rotations)
    class_sums = lax.psum_scatter(local_sums, "img", scatter_dimension=1, tiled=True)
    return (class_sums, class_weights)


def solution(mesh):
    placed = (P(("img", "ref"), None), P("ref", None), P("ref"))
    return jax.shard_map(
        per_device,
        mesh=mesh,
        in_specs=placed,
        out_specs=(P("ref", "img"), P("ref")),
        check_vma=False,
    )
```

```python
import functools

import jax
import jax.numpy as jnp
from jax import lax
from jax.experimental import pallas as pl
from jax.experimental.pallas import tpu as pltpu
from jax.sharding import PartitionSpec as P

ANG = 144
LANES = 128
GROUP_COLS = 1152


def turn_sum_kernel(classes_here, rotations, by_turn_ref, images_ref, angle_ref, out_ref, products_ref):
    shift = ANG // rotations
    width = images_ref.shape[1]
    products_ref[...] = jnp.dot(
        by_turn_ref[...], images_ref[...], preferred_element_type=jnp.float32
    )
    rows = 8 if classes_here % 8 == 0 else classes_here
    cols = GROUP_COLS if width % GROUP_COLS == 0 else width
    for row0 in range(0, classes_here, rows):
        for col0 in range(0, width, cols):
            angle = angle_ref[:, col0 : col0 + cols]
            total = products_ref[row0 : row0 + rows, col0 : col0 + cols]
            for turn_index in range(1, rotations):
                start = turn_index * classes_here + row0
                part = products_ref[start : start + rows, col0 : col0 + cols]
                step = turn_index * shift
                ahead = pltpu.roll(part, cols - step, 1)
                behind = pltpu.roll(part, ANG - step, 1)
                total = total + jnp.where(angle < ANG - step, ahead, behind)
            out_ref[0, row0 : row0 + rows, col0 : col0 + cols] = total
    mass = jnp.sum(by_turn_ref[...].astype(jnp.float32), axis=1, keepdims=True)
    class_mass = mass[0:classes_here]
    for turn_index in range(1, rotations):
        class_mass = class_mass + mass[turn_index * classes_here : (turn_index + 1) * classes_here]
    out_ref[0, :, width:] = jnp.broadcast_to(class_mass, (classes_here, LANES))


def turn_and_sum(by_turn, gathered, classes_here, rotations, chunks):
    local_refs, n = by_turn.shape
    pixels = gathered.shape[1]
    width = pixels // chunks
    angle = (jnp.arange(width, dtype=jnp.int32) % ANG).reshape(1, width)
    return pl.pallas_call(
        functools.partial(turn_sum_kernel, classes_here, rotations),
        grid=(chunks,),
        in_specs=[
            pl.BlockSpec((local_refs, n), lambda t: (0, 0)),
            pl.BlockSpec((n, width), lambda t: (0, t)),
            pl.BlockSpec((1, width), lambda t: (0, 0)),
        ],
        out_specs=pl.BlockSpec((1, classes_here, width + LANES), lambda t: (t, 0, 0)),
        out_shape=jax.ShapeDtypeStruct((chunks, classes_here, width + LANES), jnp.float32),
        scratch_shapes=[pltpu.VMEM((local_refs, width), jnp.float32)],
        compiler_params=pltpu.CompilerParams(vmem_limit_bytes=60 * 1024 * 1024),
        cost_estimate=pl.CostEstimate(
            flops=2 * local_refs * n * pixels,
            bytes_accessed=2 * local_refs * n + 2 * n * pixels + 4 * classes_here * pixels,
            transcendentals=0,
        ),
    )(by_turn, gathered, angle)


def per_device(chunks, images, references, class_prior):
    local_refs, pixels = references.shape
    classes_here = class_prior.shape[0]
    rotations = local_refs // classes_here

    half_norm = 0.5 * jnp.einsum(
        "jp,jp->j", references, references, preferred_element_type=jnp.float32
    )
    offsets = (jnp.log(class_prior)[:, None] - half_norm.reshape(classes_here, rotations)).reshape(
        local_refs
    )
    gathered = lax.all_gather(images, "ref", axis=0, tiled=True)
    products = lax.dot_general(
        gathered, references, (((1,), (1,)), ((), ())), preferred_element_type=jnp.float32
    )
    scores = products + offsets
    local_max = jnp.max(scores, axis=1)
    local_sum = jnp.sum(jnp.exp(scores - local_max[:, None]), axis=1)
    stats = lax.all_gather(jnp.stack([local_max, local_sum]), "ref", axis=0)
    top_score = jnp.max(stats[:, 0], axis=0)
    denominator = jnp.sum(stats[:, 1] * jnp.exp(stats[:, 0] - top_score[None, :]), axis=0)
    weights = (jnp.exp(scores - top_score[:, None]) / denominator[:, None]).astype(jnp.bfloat16)

    n = weights.shape[0]
    by_turn = weights.reshape(n, classes_here, rotations).transpose(2, 1, 0).reshape(local_refs, n)
    chunked = turn_and_sum(by_turn, gathered, classes_here, rotations, chunks)
    reduced = lax.psum_scatter(chunked, "img", scatter_dimension=0, tiled=True)[0]
    width = pixels // chunks
    return (reduced[:, :width], reduced[:, width])


def solution(mesh):
    placed = (P(("img", "ref"), None), P("ref", None), P("ref"))
    return jax.shard_map(
        functools.partial(per_device, mesh.shape["img"]),
        mesh=mesh,
        in_specs=placed,
        out_specs=(P("ref", "img"), P("ref")),
        check_vma=False,
    )
```

```python
import functools

import jax
import jax.numpy as jnp
from jax import lax
from jax.experimental import pallas as pl
from jax.experimental.pallas import tpu as pltpu
from jax.sharding import PartitionSpec as P

ANG = 144
LANES = 128
GROUP_COLS = 1152


def turn_sum_kernel(classes_here, rotations, by_turn_ref, images_ref, angle_ref, out_ref, products_ref):
    shift = ANG // rotations
    width = images_ref.shape[1]
    products_ref[...] = jnp.dot(
        by_turn_ref[...], images_ref[...], preferred_element_type=jnp.float32
    )
    rows = 8 if classes_here % 8 == 0 else classes_here
    cols = GROUP_COLS if width % GROUP_COLS == 0 else width
    for row0 in range(0, classes_here, rows):
        for col0 in range(0, width, cols):
            angle = angle_ref[:, col0 : col0 + cols]
            total = products_ref[row0 : row0 + rows, col0 : col0 + cols]
            for turn_index in range(1, rotations):
                start = turn_index * classes_here + row0
                part = products_ref[start : start + rows, col0 : col0 + cols]
                step = turn_index * shift
                ahead = pltpu.roll(part, cols - step, 1)
                behind = pltpu.roll(part, ANG - step, 1)
                total = total + jnp.where(angle < ANG - step, ahead, behind)
            out_ref[0, row0 : row0 + rows, col0 : col0 + cols] = total
    mass = jnp.sum(by_turn_ref[...].astype(jnp.float32), axis=1, keepdims=True)
    class_mass = mass[0:classes_here]
    for turn_index in range(1, rotations):
        class_mass = class_mass + mass[turn_index * classes_here : (turn_index + 1) * classes_here]
    out_ref[0, :, width:] = jnp.broadcast_to(class_mass, (classes_here, LANES))


def turn_and_sum(by_turn, gathered, angle, classes_here, rotations):
    local_refs, n = by_turn.shape
    width = gathered.shape[1]
    return pl.pallas_call(
        functools.partial(turn_sum_kernel, classes_here, rotations),
        grid=(1,),
        in_specs=[
            pl.BlockSpec((local_refs, n), lambda t: (0, 0)),
            pl.BlockSpec((n, width), lambda t: (0, 0)),
            pl.BlockSpec((1, width), lambda t: (0, 0)),
        ],
        out_specs=pl.BlockSpec((1, classes_here, width + LANES), lambda t: (0, 0, 0)),
        out_shape=jax.ShapeDtypeStruct((1, classes_here, width + LANES), jnp.float32),
        scratch_shapes=[pltpu.VMEM((local_refs, width), jnp.float32)],
        compiler_params=pltpu.CompilerParams(vmem_limit_bytes=60 * 1024 * 1024),
        cost_estimate=pl.CostEstimate(
            flops=2 * local_refs * n * width,
            bytes_accessed=2 * local_refs * n + 2 * n * width + 4 * classes_here * width,
            transcendentals=0,
        ),
    )(by_turn, gathered, angle)


def gather_from_all(value, axis_name, size):
    me = lax.axis_index(axis_name)
    parts = [value]
    for step in range(1, size):
        perm = [(src, (src + step) % size) for src in range(size)]
        parts.append(lax.ppermute(value, axis_name, perm))
    return parts


def per_device(n_img, n_ref, images, references, class_prior):
    local_refs, pixels = references.shape
    classes_here = class_prior.shape[0]
    rotations = local_refs // classes_here
    width = pixels // n_img

    half_norm = 0.5 * jnp.einsum(
        "jp,jp->j", references, references, preferred_element_type=jnp.float32
    )
    offsets = (jnp.log(class_prior)[:, None] - half_norm.reshape(classes_here, rotations)).reshape(
        local_refs
    )
    pieces = []
    products = None
    for chunk in range(n_img):
        cols = slice(chunk * width, (chunk + 1) * width)
        piece = lax.all_gather(images[:, cols], "ref", axis=0, tiled=True)
        pieces.append(piece)
        part = lax.dot_general(
            piece, references[:, cols], (((1,), (1,)), ((), ())), preferred_element_type=jnp.float32
        )
        products = part if products is None else products + part
    scores = products + offsets
    local_max = jnp.max(scores, axis=1)
    local_sum = jnp.sum(jnp.exp(scores - local_max[:, None]), axis=1)
    stats = gather_from_all(jnp.stack([local_max, local_sum]), "ref", n_ref)
    top_score = stats[0][0]
    for other in stats[1:]:
        top_score = jnp.maximum(top_score, other[0])
    denominator = None
    for other in stats:
        term = other[1] * jnp.exp(other[0] - top_score)
        denominator = term if denominator is None else denominator + term
    weights = (jnp.exp(scores - top_score[:, None]) / denominator[:, None]).astype(jnp.bfloat16)

    n = weights.shape[0]
    by_turn = weights.reshape(n, classes_here, rotations).transpose(2, 1, 0).reshape(local_refs, n)
    angle = (jnp.arange(width, dtype=jnp.int32) % ANG).reshape(1, width)
    chunked = jnp.concatenate(
        [turn_and_sum(by_turn, piece, angle, classes_here, rotations) for piece in pieces], axis=0
    )
    me = lax.axis_index("img")
    reduced = chunked[me]
    for step in range(1, n_img):
        perm = [(src, (src + step) % n_img) for src in range(n_img)]
        outgoing = lax.dynamic_index_in_dim(chunked, (me + step) % n_img, 0, keepdims=False)
        reduced = reduced + lax.ppermute(outgoing, "img", perm)
    return (reduced[:, :width], reduced[:, width])


def solution(mesh):
    placed = (P(("img", "ref"), None), P("ref", None), P("ref"))
    return jax.shard_map(
        functools.partial(per_device, mesh.shape["img"], mesh.shape["ref"]),
        mesh=mesh,
        in_specs=placed,
        out_specs=(P("ref", "img"), P("ref")),
        check_vma=False,
    )
```

```python
import functools

import jax
import jax.numpy as jnp
from jax import lax
from jax.experimental import pallas as pl
from jax.experimental.pallas import tpu as pltpu
from jax.sharding import PartitionSpec as P

ANG = 144
LANES = 128
GROUP_COLS = 1152


def turn_sum_kernel(classes_here, rotations, by_turn_ref, images_ref, angle_ref, out_ref, products_ref):
    shift = ANG // rotations
    width = images_ref.shape[1]
    products_ref[...] = jnp.dot(
        by_turn_ref[...], images_ref[...], preferred_element_type=jnp.float32
    )
    rows = 8 if classes_here % 8 == 0 else classes_here
    cols = GROUP_COLS if width % GROUP_COLS == 0 else width
    for row0 in range(0, classes_here, rows):
        for col0 in range(0, width, cols):
            angle = angle_ref[:, col0 : col0 + cols]
            kept = products_ref[row0 : row0 + rows, col0 : col0 + cols]
            every = None
            for turn_index in range(1, rotations):
                start = turn_index * classes_here + row0
                part = products_ref[start : start + rows, col0 : col0 + cols]
                step = turn_index * shift
                ahead = pltpu.roll(part, cols - step, 1)
                kept = kept + jnp.where(angle < ANG - step, ahead, 0.0)
                every = ahead if every is None else every + ahead
            wrapped = every - (kept - products_ref[row0 : row0 + rows, col0 : col0 + cols])
            out_ref[0, row0 : row0 + rows, col0 : col0 + cols] = kept + pltpu.roll(wrapped, ANG, 1)
    mass = jnp.sum(by_turn_ref[...].astype(jnp.float32), axis=1, keepdims=True)
    class_mass = mass[0:classes_here]
    for turn_index in range(1, rotations):
        class_mass = class_mass + mass[turn_index * classes_here : (turn_index + 1) * classes_here]
    out_ref[0, :, width:] = jnp.broadcast_to(class_mass, (classes_here, LANES))


def turn_and_sum(by_turn, gathered, classes_here, rotations, chunks):
    local_refs, n = by_turn.shape
    pixels = gathered.shape[1]
    width = pixels // chunks
    angle = (jnp.arange(width, dtype=jnp.int32) % ANG).reshape(1, width)
    return pl.pallas_call(
        functools.partial(turn_sum_kernel, classes_here, rotations),
        grid=(chunks,),
        in_specs=[
            pl.BlockSpec((local_refs, n), lambda t: (0, 0)),
            pl.BlockSpec((n, width), lambda t: (0, t)),
            pl.BlockSpec((1, width), lambda t: (0, 0)),
        ],
        out_specs=pl.BlockSpec((1, classes_here, width + LANES), lambda t: (t, 0, 0)),
        out_shape=jax.ShapeDtypeStruct((chunks, classes_here, width + LANES), jnp.float32),
        scratch_shapes=[pltpu.VMEM((local_refs, width), jnp.float32)],
        compiler_params=pltpu.CompilerParams(vmem_limit_bytes=60 * 1024 * 1024),
        cost_estimate=pl.CostEstimate(
            flops=2 * local_refs * n * pixels,
            bytes_accessed=2 * local_refs * n + 2 * n * pixels + 4 * classes_here * pixels,
            transcendentals=0,
        ),
    )(by_turn, gathered, angle)


def per_device(chunks, images, references, class_prior):
    local_refs, pixels = references.shape
    classes_here = class_prior.shape[0]
    rotations = local_refs // classes_here

    half_norm = 0.5 * jnp.einsum(
        "jp,jp->j", references, references, preferred_element_type=jnp.float32
    )
    offsets = (jnp.log(class_prior)[:, None] - half_norm.reshape(classes_here, rotations)).reshape(
        local_refs
    )
    gathered = lax.all_gather(images, "ref", axis=0, tiled=True)
    products = lax.dot_general(
        gathered, references, (((1,), (1,)), ((), ())), preferred_element_type=jnp.float32
    )
    scores = products + offsets
    local_max = jnp.max(scores, axis=1)
    local_sum = jnp.sum(jnp.exp(scores - local_max[:, None]), axis=1)
    stats = lax.all_gather(jnp.stack([local_max, local_sum]), "ref", axis=0)
    top_score = jnp.max(stats[:, 0], axis=0)
    denominator = jnp.sum(stats[:, 1] * jnp.exp(stats[:, 0] - top_score[None, :]), axis=0)
    weights = (jnp.exp(scores - top_score[:, None]) / denominator[:, None]).astype(jnp.bfloat16)

    n = weights.shape[0]
    by_turn = weights.reshape(n, classes_here, rotations).transpose(2, 1, 0).reshape(local_refs, n)
    chunked = turn_and_sum(by_turn, gathered, classes_here, rotations, chunks)
    reduced = lax.psum_scatter(chunked, "img", scatter_dimension=0, tiled=True)[0]
    width = pixels // chunks
    return (reduced[:, :width], reduced[:, width])


def solution(mesh):
    placed = (P(("img", "ref"), None), P("ref", None), P("ref"))
    return jax.shard_map(
        functools.partial(per_device, mesh.shape["img"]),
        mesh=mesh,
        in_specs=placed,
        out_specs=(P("ref", "img"), P("ref")),
        check_vma=False,
    )
```

```python
import functools

import jax
import jax.numpy as jnp
from jax import lax
from jax.experimental import pallas as pl
from jax.experimental.pallas import tpu as pltpu
from jax.sharding import PartitionSpec as P

ANG = 144
LANES = 128
GROUP_COLS = 1152


def turn_sum_kernel(
    classes_here, rotations, by_turn_ref, own_ref, partner_ref, angle_ref, out_ref, products_ref
):
    shift = ANG // rotations
    width = own_ref.shape[1]
    half = own_ref.shape[0]
    products_ref[...] = jnp.dot(
        by_turn_ref[:, 0:half], own_ref[...], preferred_element_type=jnp.float32
    ) + jnp.dot(by_turn_ref[:, half:], partner_ref[...], preferred_element_type=jnp.float32)
    rows = 8 if classes_here % 8 == 0 else classes_here
    cols = GROUP_COLS if width % GROUP_COLS == 0 else width
    for row0 in range(0, classes_here, rows):
        for col0 in range(0, width, cols):
            angle = angle_ref[:, col0 : col0 + cols]
            kept = products_ref[row0 : row0 + rows, col0 : col0 + cols]
            every = None
            for turn_index in range(1, rotations):
                start = turn_index * classes_here + row0
                part = products_ref[start : start + rows, col0 : col0 + cols]
                step = turn_index * shift
                ahead = pltpu.roll(part, cols - step, 1)
                kept = kept + jnp.where(angle < ANG - step, ahead, 0.0)
                every = ahead if every is None else every + ahead
            wrapped = every - (kept - products_ref[row0 : row0 + rows, col0 : col0 + cols])
            out_ref[0, row0 : row0 + rows, col0 : col0 + cols] = kept + pltpu.roll(wrapped, ANG, 1)
    mass = jnp.sum(by_turn_ref[...].astype(jnp.float32), axis=1, keepdims=True)
    class_mass = mass[0:classes_here]
    for turn_index in range(1, rotations):
        class_mass = class_mass + mass[turn_index * classes_here : (turn_index + 1) * classes_here]
    out_ref[0, :, width:] = jnp.broadcast_to(class_mass, (classes_here, LANES))


def turn_and_sum(by_turn, own, partner, classes_here, rotations, chunks):
    local_refs, n = by_turn.shape
    half, pixels = own.shape
    width = pixels // chunks
    angle = (jnp.arange(width, dtype=jnp.int32) % ANG).reshape(1, width)
    return pl.pallas_call(
        functools.partial(turn_sum_kernel, classes_here, rotations),
        grid=(chunks,),
        in_specs=[
            pl.BlockSpec((local_refs, n), lambda t: (0, 0)),
            pl.BlockSpec((half, width), lambda t: (0, t)),
            pl.BlockSpec((half, width), lambda t: (0, t)),
            pl.BlockSpec((1, width), lambda t: (0, 0)),
        ],
        out_specs=pl.BlockSpec((1, classes_here, width + LANES), lambda t: (t, 0, 0)),
        out_shape=jax.ShapeDtypeStruct((chunks, classes_here, width + LANES), jnp.float32),
        scratch_shapes=[pltpu.VMEM((local_refs, width), jnp.float32)],
        compiler_params=pltpu.CompilerParams(vmem_limit_bytes=60 * 1024 * 1024),
        cost_estimate=pl.CostEstimate(
            flops=2 * local_refs * n * pixels,
            bytes_accessed=2 * local_refs * n + 2 * n * pixels + 4 * classes_here * pixels,
            transcendentals=0,
        ),
    )(by_turn, own, partner, angle)


def per_device(chunks, n_ref, images, references, class_prior):
    local_refs, pixels = references.shape
    classes_here = class_prior.shape[0]
    rotations = local_refs // classes_here

    half_norm = 0.5 * jnp.einsum(
        "jp,jp->j", references, references, preferred_element_type=jnp.float32
    )
    offsets = (jnp.log(class_prior)[:, None] - half_norm.reshape(classes_here, rotations)).reshape(
        local_refs
    )
    core = lax.axis_index("ref") % 2
    same_core = [[c + 2 * i for i in range(n_ref // 2)] for c in range(2)]
    own = lax.all_gather(images, "ref", axis=0, tiled=True, axis_index_groups=same_core)
    partner = lax.ppermute(own, "ref", [(d, d ^ 1) for d in range(n_ref)])

    def scores_of(block):
        products = lax.dot_general(
            block, references, (((1,), (1,)), ((), ())), preferred_element_type=jnp.float32
        )
        return products + offsets

    own_scores = scores_of(own)
    partner_scores = scores_of(partner)

    def local_stats(scores):
        local_max = jnp.max(scores, axis=1)
        return jnp.stack([local_max, jnp.sum(jnp.exp(scores - local_max[:, None]), axis=1)])

    mine, theirs = local_stats(own_scores), local_stats(partner_scores)
    common = jnp.where(core == 0, jnp.concatenate([mine, theirs], 1), jnp.concatenate([theirs, mine], 1))
    stats = lax.all_gather(common, "ref", axis=0)
    top_score = jnp.max(stats[:, 0], axis=0)
    denominator = jnp.sum(stats[:, 1] * jnp.exp(stats[:, 0] - top_score[None, :]), axis=0)
    half = own.shape[0]
    norm = jnp.stack([top_score, denominator])
    norm = jnp.where(core == 0, norm, jnp.concatenate([norm[:, half:], norm[:, :half]], 1))

    def weights_of(scores, part):
        return (jnp.exp(scores - part[0][:, None]) / part[1][:, None]).astype(jnp.bfloat16)

    weights = jnp.concatenate(
        [weights_of(own_scores, norm[:, :half]), weights_of(partner_scores, norm[:, half:])], axis=0
    )

    n = weights.shape[0]
    by_turn = weights.reshape(n, classes_here, rotations).transpose(2, 1, 0).reshape(local_refs, n)
    chunked = turn_and_sum(by_turn, own, partner, classes_here, rotations, chunks)
    reduced = lax.psum_scatter(chunked, "img", scatter_dimension=0, tiled=True)[0]
    width = pixels // chunks
    return (reduced[:, :width], reduced[:, width])


def solution(mesh):
    placed = (P(("img", "ref"), None), P("ref", None), P("ref"))
    return jax.shard_map(
        functools.partial(per_device, mesh.shape["img"], mesh.shape["ref"]),
        mesh=mesh,
        in_specs=placed,
        out_specs=(P("ref", "img"), P("ref")),
        check_vma=False,
    )
```

```python
import functools

import jax
import jax.numpy as jnp
from jax import lax
from jax.experimental import pallas as pl
from jax.experimental.pallas import tpu as pltpu
from jax.sharding import PartitionSpec as P

ANG = 144
LANES = 128
GROUP_COLS = 1152


def turn_sum_kernel(classes_here, rotations, by_turn_ref, images_ref, angle_ref, out_ref, products_ref):
    shift = ANG // rotations
    width = images_ref.shape[1]
    products_ref[...] = jnp.dot(
        by_turn_ref[...], images_ref[...], preferred_element_type=jnp.float32
    )
    rows = 8 if classes_here % 8 == 0 else classes_here
    cols = GROUP_COLS if width % GROUP_COLS == 0 else width
    for row0 in range(0, classes_here, rows):
        for col0 in range(0, width, cols):
            angle = angle_ref[:, col0 : col0 + cols]
            kept = products_ref[row0 : row0 + rows, col0 : col0 + cols]
            every = None
            for turn_index in range(1, rotations):
                start = turn_index * classes_here + row0
                part = products_ref[start : start + rows, col0 : col0 + cols]
                step = turn_index * shift
                ahead = pltpu.roll(part, cols - step, 1)
                kept = kept + jnp.where(angle < ANG - step, ahead, 0.0)
                every = ahead if every is None else every + ahead
            wrapped = every - (kept - products_ref[row0 : row0 + rows, col0 : col0 + cols])
            out_ref[0, row0 : row0 + rows, col0 : col0 + cols] = kept + pltpu.roll(wrapped, ANG, 1)


def turn_and_sum(by_turn, gathered, classes_here, rotations, chunks):
    local_refs, n = by_turn.shape
    pixels = gathered.shape[1]
    width = pixels // chunks
    angle = (jnp.arange(width, dtype=jnp.int32) % ANG).reshape(1, width)
    return pl.pallas_call(
        functools.partial(turn_sum_kernel, classes_here, rotations),
        grid=(chunks,),
        in_specs=[
            pl.BlockSpec((local_refs, n), lambda t: (0, 0)),
            pl.BlockSpec((n, width), lambda t: (0, t)),
            pl.BlockSpec((1, width), lambda t: (0, 0)),
        ],
        out_specs=pl.BlockSpec((1, classes_here, width), lambda t: (t, 0, 0)),
        out_shape=jax.ShapeDtypeStruct((chunks, classes_here, width), jnp.float32),
        scratch_shapes=[pltpu.VMEM((local_refs, width), jnp.float32)],
        compiler_params=pltpu.CompilerParams(vmem_limit_bytes=60 * 1024 * 1024),
        cost_estimate=pl.CostEstimate(
            flops=2 * local_refs * n * pixels,
            bytes_accessed=2 * local_refs * n + 2 * n * pixels + 4 * classes_here * pixels,
            transcendentals=0,
        ),
    )(by_turn, gathered, angle)


def per_device(chunks, images, references, class_prior):
    local_refs, pixels = references.shape
    classes_here = class_prior.shape[0]
    rotations = local_refs // classes_here

    half_norm = 0.5 * jnp.einsum(
        "jp,jp->j", references, references, preferred_element_type=jnp.float32
    )
    offsets = (jnp.log(class_prior)[:, None] - half_norm.reshape(classes_here, rotations)).reshape(
        local_refs
    )
    gathered = lax.all_gather(images, "ref", axis=0, tiled=True)
    products = lax.dot_general(
        gathered, references, (((1,), (1,)), ((), ())), preferred_element_type=jnp.float32
    )
    scores = products + offsets
    local_max = jnp.max(scores, axis=1)
    local_sum = jnp.sum(jnp.exp(scores - local_max[:, None]), axis=1)
    stats = lax.all_gather(jnp.stack([local_max, local_sum]), "ref", axis=0)
    top_score = jnp.max(stats[:, 0], axis=0)
    denominator = jnp.sum(stats[:, 1] * jnp.exp(stats[:, 0] - top_score[None, :]), axis=0)
    weights = (jnp.exp(scores - top_score[:, None]) / denominator[:, None]).astype(jnp.bfloat16)

    n = weights.shape[0]
    by_turn = weights.reshape(n, classes_here, rotations).transpose(2, 1, 0).reshape(local_refs, n)
    local_mass = (
        jnp.sum(weights.astype(jnp.float32), axis=0).reshape(classes_here, rotations).sum(axis=1)
    )
    class_weights = local_mass
    for step in range(1, chunks):
        perm = [(src, (src + step) % chunks) for src in range(chunks)]
        class_weights = class_weights + lax.ppermute(local_mass, "img", perm)
    chunked = turn_and_sum(by_turn, gathered, classes_here, rotations, chunks)
    class_sums = lax.psum_scatter(chunked, "img", scatter_dimension=0, tiled=True)
    return (class_sums[0], class_weights)

def solution(mesh):
    placed = (P(("img", "ref"), None), P("ref", None), P("ref"))
    return jax.shard_map(
        functools.partial(per_device, mesh.shape["img"]),
        mesh=mesh,
        in_specs=placed,
        out_specs=(P("ref", "img"), P("ref")),
        check_vma=False,
    )
```

```python
import functools

import jax
import jax.numpy as jnp
from jax import lax
from jax.experimental import pallas as pl
from jax.experimental.pallas import tpu as pltpu
from jax.sharding import PartitionSpec as P

ANG = 144
LANES = 128
GROUP_COLS = 1152


def turn_sum_kernel(classes_here, rotations, by_turn_ref, images_ref, angle_ref, out_ref, products_ref):
    shift = ANG // rotations
    width = images_ref.shape[1]
    products_ref[...] = jnp.dot(
        by_turn_ref[...], images_ref[...], preferred_element_type=jnp.float32
    )
    rows = 8 if classes_here % 8 == 0 else classes_here
    cols = GROUP_COLS if width % GROUP_COLS == 0 else width
    for row0 in range(0, classes_here, rows):
        for col0 in range(0, width, cols):
            angle = angle_ref[:, col0 : col0 + cols]
            kept = products_ref[row0 : row0 + rows, col0 : col0 + cols]
            every = None
            for turn_index in range(1, rotations):
                start = turn_index * classes_here + row0
                part = products_ref[start : start + rows, col0 : col0 + cols]
                step = turn_index * shift
                ahead = pltpu.roll(part, cols - step, 1)
                kept = kept + jnp.where(angle < ANG - step, ahead, 0.0)
                every = ahead if every is None else every + ahead
            wrapped = every - (kept - products_ref[row0 : row0 + rows, col0 : col0 + cols])
            out_ref[0, row0 : row0 + rows, col0 : col0 + cols] = kept + pltpu.roll(wrapped, ANG, 1)


def turn_and_sum(by_turn, gathered, classes_here, rotations, chunks):
    local_refs, n = by_turn.shape
    pixels = gathered.shape[1]
    width = pixels // chunks
    angle = (jnp.arange(width, dtype=jnp.int32) % ANG).reshape(1, width)
    return pl.pallas_call(
        functools.partial(turn_sum_kernel, classes_here, rotations),
        grid=(chunks,),
        in_specs=[
            pl.BlockSpec((local_refs, n), lambda t: (0, 0)),
            pl.BlockSpec((n, width), lambda t: (0, t)),
            pl.BlockSpec((1, width), lambda t: (0, 0)),
        ],
        out_specs=pl.BlockSpec((1, classes_here, width), lambda t: (t, 0, 0)),
        out_shape=jax.ShapeDtypeStruct((chunks, classes_here, width), jnp.float32),
        scratch_shapes=[pltpu.VMEM((local_refs, width), jnp.float32)],
        compiler_params=pltpu.CompilerParams(vmem_limit_bytes=60 * 1024 * 1024),
        cost_estimate=pl.CostEstimate(
            flops=2 * local_refs * n * pixels,
            bytes_accessed=2 * local_refs * n + 2 * n * pixels + 4 * classes_here * pixels,
            transcendentals=0,
        ),
    )(by_turn, gathered, angle)


def score_kernel(images_ref, references_ref, offsets_ref, out_ref, acc_ref):
    step = pl.program_id(0)

    @pl.when(step == 0)
    def _():
        acc_ref[...] = jnp.zeros_like(acc_ref)

    acc_ref[...] += lax.dot_general(
        images_ref[...], references_ref[...], (((1,), (1,)), ((), ())),
        preferred_element_type=jnp.float32,
    )

    @pl.when(step == pl.num_programs(0) - 1)
    def _():
        out_ref[...] = acc_ref[...] + offsets_ref[...]


def scores_of(gathered, references, offsets):
    n, pixels = gathered.shape
    local_refs = references.shape[0]
    depth = GROUP_COLS if pixels % GROUP_COLS == 0 else pixels
    return pl.pallas_call(
        score_kernel,
        grid=(pixels // depth,),
        in_specs=[
            pl.BlockSpec((n, depth), lambda k: (0, k)),
            pl.BlockSpec((local_refs, depth), lambda k: (0, k)),
            pl.BlockSpec((1, local_refs), lambda k: (0, 0)),
        ],
        out_specs=pl.BlockSpec((n, local_refs), lambda k: (0, 0)),
        out_shape=jax.ShapeDtypeStruct((n, local_refs), jnp.float32),
        scratch_shapes=[pltpu.VMEM((n, local_refs), jnp.float32)],
        compiler_params=pltpu.CompilerParams(vmem_limit_bytes=60 * 1024 * 1024),
        cost_estimate=pl.CostEstimate(
            flops=2 * n * local_refs * pixels,
            bytes_accessed=2 * n * pixels + 2 * local_refs * pixels + 4 * n * local_refs,
            transcendentals=0,
        ),
    )(gathered, references, offsets.reshape(1, local_refs))


def per_device(chunks, images, references, class_prior):
    local_refs, pixels = references.shape
    classes_here = class_prior.shape[0]
    rotations = local_refs // classes_here

    half_norm = 0.5 * jnp.einsum(
        "jp,jp->j", references, references, preferred_element_type=jnp.float32
    )
    offsets = (jnp.log(class_prior)[:, None] - half_norm.reshape(classes_here, rotations)).reshape(
        local_refs
    )
    gathered = lax.all_gather(images, "ref", axis=0, tiled=True)
    scores = scores_of(gathered, references, offsets)
    local_max = jnp.max(scores, axis=1)
    local_sum = jnp.sum(jnp.exp(scores - local_max[:, None]), axis=1)
    stats = lax.all_gather(jnp.stack([local_max, local_sum]), "ref", axis=0)
    top_score = jnp.max(stats[:, 0], axis=0)
    denominator = jnp.sum(stats[:, 1] * jnp.exp(stats[:, 0] - top_score[None, :]), axis=0)
    weights = (jnp.exp(scores - top_score[:, None]) / denominator[:, None]).astype(jnp.bfloat16)

    n = weights.shape[0]
    by_turn = weights.reshape(n, classes_here, rotations).transpose(2, 1, 0).reshape(local_refs, n)
    local_mass = (
        jnp.sum(weights.astype(jnp.float32), axis=0).reshape(classes_here, rotations).sum(axis=1)
    )
    class_weights = local_mass
    for step in range(1, chunks):
        perm = [(src, (src + step) % chunks) for src in range(chunks)]
        class_weights = class_weights + lax.ppermute(local_mass, "img", perm)
    chunked = turn_and_sum(by_turn, gathered, classes_here, rotations, chunks)
    class_sums = lax.psum_scatter(chunked, "img", scatter_dimension=0, tiled=True)
    return (class_sums[0], class_weights)

def solution(mesh):
    placed = (P(("img", "ref"), None), P("ref", None), P("ref"))
    return jax.shard_map(
        functools.partial(per_device, mesh.shape["img"]),
        mesh=mesh,
        in_specs=placed,
        out_specs=(P("ref", "img"), P("ref")),
        check_vma=False,
    )
```

```python
import functools

import jax
import numpy as np
import jax.numpy as jnp
from jax import lax
from jax.experimental import pallas as pl
from jax.experimental.pallas import tpu as pltpu
from jax.sharding import PartitionSpec as P

ANG = 144
LANES = 128
GROUP_COLS = 1152


def turn_sum_kernel(classes_here, rotations, by_turn_ref, images_ref, angle_ref, out_ref, products_ref):
    shift = ANG // rotations
    width = images_ref.shape[1]
    products_ref[...] = jnp.dot(
        by_turn_ref[...], images_ref[...], preferred_element_type=jnp.float32
    )
    rows = 8 if classes_here % 8 == 0 else classes_here
    cols = GROUP_COLS if width % GROUP_COLS == 0 else width
    for row0 in range(0, classes_here, rows):
        for col0 in range(0, width, cols):
            angle = angle_ref[:, col0 : col0 + cols]
            kept = products_ref[row0 : row0 + rows, col0 : col0 + cols]
            every = None
            for turn_index in range(1, rotations):
                start = turn_index * classes_here + row0
                part = products_ref[start : start + rows, col0 : col0 + cols]
                step = turn_index * shift
                ahead = pltpu.roll(part, cols - step, 1)
                kept = kept + jnp.where(angle < ANG - step, ahead, 0.0)
                every = ahead if every is None else every + ahead
            wrapped = every - (kept - products_ref[row0 : row0 + rows, col0 : col0 + cols])
            out_ref[0, row0 : row0 + rows, col0 : col0 + cols] = kept + pltpu.roll(wrapped, ANG, 1)


def turn_and_sum(by_turn, gathered, classes_here, rotations, chunks):
    local_refs, n = by_turn.shape
    pixels = gathered.shape[1]
    width = pixels // chunks
    angle = (jnp.arange(width, dtype=jnp.int32) % ANG).reshape(1, width)
    return pl.pallas_call(
        functools.partial(turn_sum_kernel, classes_here, rotations),
        grid=(chunks,),
        in_specs=[
            pl.BlockSpec((local_refs, n), lambda t: (0, 0)),
            pl.BlockSpec((n, width), lambda t: (0, t)),
            pl.BlockSpec((1, width), lambda t: (0, 0)),
        ],
        out_specs=pl.BlockSpec((1, classes_here, width), lambda t: (t, 0, 0)),
        out_shape=jax.ShapeDtypeStruct((chunks, classes_here, width), jnp.float32),
        scratch_shapes=[pltpu.VMEM((local_refs, width), jnp.float32)],
        compiler_params=pltpu.CompilerParams(vmem_limit_bytes=60 * 1024 * 1024),
        cost_estimate=pl.CostEstimate(
            flops=2 * local_refs * n * pixels,
            bytes_accessed=2 * local_refs * n + 2 * n * pixels + 4 * classes_here * pixels,
            transcendentals=0,
        ),
    )(by_turn, gathered, angle)


def ring_order(chips):
    if chips == 4:
        return [0, 1, 3, 2]
    order = []
    for row in range(chips // 2):
        order += [2 * row, 2 * row + 1] if row % 2 == 0 else [2 * row + 1, 2 * row]
    return order


def ring_gather(images, n_ref):
    chips = n_ref // 2
    block = images.shape[0]
    ring = ring_order(chips)
    place = {chip: i for i, chip in enumerate(ring)}

    def ahead(chip, hops):
        return ring[(place[chip] + hops) % chips]

    to_next = [(2 * c + k, 2 * ahead(c, 1) + k) for c in range(chips) for k in range(2)]
    to_prev = [(2 * c + k, 2 * ahead(c, -1) + k) for c in range(chips) for k in range(2)]
    to_partner = [(d, d ^ 1) for d in range(n_ref)]
    pieces = [(images, 0, 0, block)]
    from_prev = images
    from_next = images
    for hops in range(1, (chips + 1) // 2):
        from_prev = lax.ppermute(from_prev, "ref", to_next)
        from_next = lax.ppermute(from_next, "ref", to_prev)
        pieces += [(from_prev, -hops, 0, block), (from_next, hops, 0, block)]
    if chips % 2 == 0:
        half = block // 2
        top = lax.ppermute(from_prev[:half], "ref", to_next)
        bottom = lax.ppermute(from_next[half:], "ref", to_prev)
        pieces += [(top, chips // 2, 0, half), (bottom, chips // 2, half, block - half)]
    arrays = [piece[0] for piece in pieces]
    arrays += [lax.ppermute(piece[0], "ref", to_partner) for piece in pieces]
    table = []
    for device in range(n_ref):
        chip, core = device // 2, device % 2
        rows = []
        for side in (core, 1 - core):
            for _, hops, first, count in pieces:
                origin = 2 * ahead(chip, hops) + side
                rows += list(range(origin * block + first, origin * block + first + count))
        table.append(rows)
    return jnp.concatenate(arrays, axis=0), np.array(table, np.int32)


def per_device(chunks, n_ref, images, references, class_prior):
    local_refs, pixels = references.shape
    classes_here = class_prior.shape[0]
    rotations = local_refs // classes_here

    half_norm = 0.5 * jnp.einsum(
        "jp,jp->j", references, references, preferred_element_type=jnp.float32
    )
    offsets = (jnp.log(class_prior)[:, None] - half_norm.reshape(classes_here, rotations)).reshape(
        local_refs
    )
    gathered, table = ring_gather(images, n_ref)
    to_group = jnp.asarray(table)[lax.axis_index("ref")]
    from_group = jnp.asarray(np.argsort(table, axis=1).astype(np.int32))[lax.axis_index("ref")]
    products = lax.dot_general(
        gathered, references, (((1,), (1,)), ((), ())), preferred_element_type=jnp.float32
    )
    scores = products + offsets
    local_max = jnp.max(scores, axis=1)
    local_sum = jnp.sum(jnp.exp(scores - local_max[:, None]), axis=1)
    in_group_order = jnp.take(jnp.stack([local_max, local_sum]), from_group, axis=1)
    stats = lax.all_gather(in_group_order, "ref", axis=0)
    top_score = jnp.max(stats[:, 0], axis=0)
    denominator = jnp.sum(stats[:, 1] * jnp.exp(stats[:, 0] - top_score[None, :]), axis=0)
    norm = jnp.take(jnp.stack([top_score, denominator]), to_group, axis=1)
    top_score, denominator = norm[0], norm[1]
    weights = (jnp.exp(scores - top_score[:, None]) / denominator[:, None]).astype(jnp.bfloat16)

    n = weights.shape[0]
    by_turn = weights.reshape(n, classes_here, rotations).transpose(2, 1, 0).reshape(local_refs, n)
    local_mass = (
        jnp.sum(weights.astype(jnp.float32), axis=0).reshape(classes_here, rotations).sum(axis=1)
    )
    class_weights = local_mass
    for step in range(1, chunks):
        perm = [(src, (src + step) % chunks) for src in range(chunks)]
        class_weights = class_weights + lax.ppermute(local_mass, "img", perm)
    chunked = turn_and_sum(by_turn, gathered, classes_here, rotations, chunks)
    class_sums = lax.psum_scatter(chunked, "img", scatter_dimension=0, tiled=True)
    return (class_sums[0], class_weights)

def solution(mesh):
    placed = (P(("img", "ref"), None), P("ref", None), P("ref"))
    return jax.shard_map(
        functools.partial(per_device, mesh.shape["img"], mesh.shape["ref"]),
        mesh=mesh,
        in_specs=placed,
        out_specs=(P("ref", "img"), P("ref")),
        check_vma=False,
    )
```

```python
import functools

import jax
import numpy as np
import jax.numpy as jnp
from jax import lax
from jax.experimental import pallas as pl
from jax.experimental.pallas import tpu as pltpu
from jax.sharding import PartitionSpec as P

ANG = 144
LANES = 128
GROUP_COLS = 1152


def turn_sum_kernel(classes_here, rotations, by_turn_ref, images_ref, angle_ref, out_ref, products_ref):
    shift = ANG // rotations
    width = images_ref.shape[1]
    products_ref[...] = jnp.dot(
        by_turn_ref[...], images_ref[...], preferred_element_type=jnp.float32
    )
    rows = 8 if classes_here % 8 == 0 else classes_here
    cols = GROUP_COLS if width % GROUP_COLS == 0 else width
    for row0 in range(0, classes_here, rows):
        for col0 in range(0, width, cols):
            angle = angle_ref[:, col0 : col0 + cols]
            kept = products_ref[row0 : row0 + rows, col0 : col0 + cols]
            every = None
            for turn_index in range(1, rotations):
                start = turn_index * classes_here + row0
                part = products_ref[start : start + rows, col0 : col0 + cols]
                step = turn_index * shift
                ahead = pltpu.roll(part, cols - step, 1)
                kept = kept + jnp.where(angle < ANG - step, ahead, 0.0)
                every = ahead if every is None else every + ahead
            wrapped = every - (kept - products_ref[row0 : row0 + rows, col0 : col0 + cols])
            out_ref[0, row0 : row0 + rows, col0 : col0 + cols] = kept + pltpu.roll(wrapped, ANG, 1)


def turn_and_sum(by_turn, gathered, classes_here, rotations, chunks):
    local_refs, n = by_turn.shape
    pixels = gathered.shape[1]
    width = pixels // chunks
    angle = (jnp.arange(width, dtype=jnp.int32) % ANG).reshape(1, width)
    return pl.pallas_call(
        functools.partial(turn_sum_kernel, classes_here, rotations),
        grid=(chunks,),
        in_specs=[
            pl.BlockSpec((local_refs, n), lambda t: (0, 0)),
            pl.BlockSpec((n, width), lambda t: (0, t)),
            pl.BlockSpec((1, width), lambda t: (0, 0)),
        ],
        out_specs=pl.BlockSpec((1, classes_here, width), lambda t: (t, 0, 0)),
        out_shape=jax.ShapeDtypeStruct((chunks, classes_here, width), jnp.float32),
        scratch_shapes=[pltpu.VMEM((local_refs, width), jnp.float32)],
        compiler_params=pltpu.CompilerParams(vmem_limit_bytes=60 * 1024 * 1024),
        cost_estimate=pl.CostEstimate(
            flops=2 * local_refs * n * pixels,
            bytes_accessed=2 * local_refs * n + 2 * n * pixels + 4 * classes_here * pixels,
            transcendentals=0,
        ),
    )(by_turn, gathered, angle)


def ring_order(chips):
    if chips == 4:
        return [0, 1, 3, 2]
    order = []
    for row in range(chips // 2):
        order += [2 * row, 2 * row + 1] if row % 2 == 0 else [2 * row + 1, 2 * row]
    return order


def ring_gather(images, n_ref):
    chips = n_ref // 2
    block = images.shape[0]
    ring = ring_order(chips)
    place = {chip: i for i, chip in enumerate(ring)}

    def ahead(chip, hops):
        return ring[(place[chip] + hops) % chips]

    to_next = [(2 * c + k, 2 * ahead(c, 1) + k) for c in range(chips) for k in range(2)]
    to_prev = [(2 * c + k, 2 * ahead(c, -1) + k) for c in range(chips) for k in range(2)]
    to_partner = [(d, d ^ 1) for d in range(n_ref)]
    pieces = [(images, 0, 0, block)]
    from_prev = images
    from_next = images
    for hops in range(1, (chips + 1) // 2):
        from_prev = lax.ppermute(from_prev, "ref", to_next)
        from_next = lax.ppermute(from_next, "ref", to_prev)
        pieces += [(from_prev, -hops, 0, block), (from_next, hops, 0, block)]
    if chips % 2 == 0:
        half = block // 2
        top = lax.ppermute(from_prev[:half], "ref", to_next)
        bottom = lax.ppermute(from_next[half:], "ref", to_prev)
        pieces += [(top, chips // 2, 0, half), (bottom, chips // 2, half, block - half)]
    arrays = [piece[0] for piece in pieces]
    arrays += [lax.ppermute(piece[0], "ref", to_partner) for piece in pieces]
    table = []
    for device in range(n_ref):
        chip, core = device // 2, device % 2
        rows = []
        for side in (core, 1 - core):
            for _, hops, first, count in pieces:
                origin = 2 * ahead(chip, hops) + side
                rows += list(range(origin * block + first, origin * block + first + count))
        table.append(rows)
    return jnp.concatenate(arrays, axis=0), np.array(table, np.int32)


def per_device(chunks, n_ref, images, references, class_prior):
    local_refs, pixels = references.shape
    classes_here = class_prior.shape[0]
    rotations = local_refs // classes_here

    half_norm = 0.5 * jnp.einsum(
        "jp,jp->j", references, references, preferred_element_type=jnp.float32
    )
    offsets = (jnp.log(class_prior)[:, None] - half_norm.reshape(classes_here, rotations)).reshape(
        local_refs
    )
    gathered, table = ring_gather(images, n_ref)
    to_group = jnp.asarray(table)[lax.axis_index("ref")]
    from_group = jnp.asarray(np.argsort(table, axis=1).astype(np.int32))[lax.axis_index("ref")]
    products = lax.dot_general(
        gathered, references, (((1,), (1,)), ((), ())), preferred_element_type=jnp.float32
    )
    scores = products + offsets
    local_max = jnp.max(scores, axis=1)
    local_sum = jnp.sum(jnp.exp(scores - local_max[:, None]), axis=1)
    in_group_order = jnp.take(jnp.stack([local_max, local_sum]), from_group, axis=1)
    stats = lax.all_gather(in_group_order, "ref", axis=0)
    top_score = jnp.max(stats[:, 0], axis=0)
    denominator = jnp.sum(stats[:, 1] * jnp.exp(stats[:, 0] - top_score[None, :]), axis=0)
    norm = jnp.take(jnp.stack([top_score, denominator]), to_group, axis=1)
    top_score, denominator = norm[0], norm[1]
    weights = (jnp.exp(scores - top_score[:, None]) / denominator[:, None]).astype(jnp.bfloat16)

    n = weights.shape[0]
    by_turn = weights.reshape(n, classes_here, rotations).transpose(2, 1, 0).reshape(local_refs, n)
    local_mass = (
        jnp.sum(weights.astype(jnp.float32), axis=0).reshape(classes_here, rotations).sum(axis=1)
    )
    class_weights = local_mass
    for step in range(1, chunks):
        perm = [(src, (src + step) % chunks) for src in range(chunks)]
        class_weights = class_weights + lax.ppermute(local_mass, "img", perm)
    chunked = turn_and_sum(by_turn, gathered, classes_here, rotations, chunks)
    me = lax.axis_index("img")
    class_sums = lax.dynamic_index_in_dim(chunked, me, 0, keepdims=False)
    for step in range(1, chunks):
        perm = [(src, (src + step) % chunks) for src in range(chunks)]
        outgoing = lax.dynamic_index_in_dim(chunked, (me + step) % chunks, 0, keepdims=False)
        class_sums = class_sums + lax.ppermute(outgoing, "img", perm)
    return (class_sums, class_weights)

def solution(mesh):
    placed = (P(("img", "ref"), None), P("ref", None), P("ref"))
    return jax.shard_map(
        functools.partial(per_device, mesh.shape["img"], mesh.shape["ref"]),
        mesh=mesh,
        in_specs=placed,
        out_specs=(P("ref", "img"), P("ref")),
        check_vma=False,
    )
```

```python
import functools

import jax
import numpy as np
import jax.numpy as jnp
from jax import lax
from jax.experimental import pallas as pl
from jax.experimental.pallas import tpu as pltpu
from jax.sharding import PartitionSpec as P

ANG = 144
LANES = 128
GROUP_COLS = 1152


def turn_sum_kernel(classes_here, rotations, by_turn_ref, images_ref, angle_ref, out_ref, products_ref):
    shift = ANG // rotations
    width = images_ref.shape[1]
    products_ref[...] = jnp.dot(
        by_turn_ref[...], images_ref[...], preferred_element_type=jnp.float32
    )
    rows = 8 if classes_here % 8 == 0 else classes_here
    cols = GROUP_COLS if width % GROUP_COLS == 0 else width
    for row0 in range(0, classes_here, rows):
        for col0 in range(0, width, cols):
            angle = angle_ref[:, col0 : col0 + cols]
            kept = products_ref[row0 : row0 + rows, col0 : col0 + cols]
            every = None
            for turn_index in range(1, rotations):
                start = turn_index * classes_here + row0
                part = products_ref[start : start + rows, col0 : col0 + cols]
                step = turn_index * shift
                ahead = pltpu.roll(part, cols - step, 1)
                kept = kept + jnp.where(angle < ANG - step, ahead, 0.0)
                every = ahead if every is None else every + ahead
            wrapped = every - (kept - products_ref[row0 : row0 + rows, col0 : col0 + cols])
            out_ref[0, row0 : row0 + rows, col0 : col0 + cols] = kept + pltpu.roll(wrapped, ANG, 1)
    mass = jnp.sum(by_turn_ref[...].astype(jnp.float32), axis=1, keepdims=True)
    class_mass = mass[0:classes_here]
    for turn_index in range(1, rotations):
        class_mass = class_mass + mass[turn_index * classes_here : (turn_index + 1) * classes_here]
    out_ref[0, :, width:] = jnp.broadcast_to(class_mass, (classes_here, LANES))


def turn_and_sum(by_turn, gathered, classes_here, rotations, chunks):
    local_refs, n = by_turn.shape
    pixels = gathered.shape[1]
    width = pixels // chunks
    angle = (jnp.arange(width, dtype=jnp.int32) % ANG).reshape(1, width)
    return pl.pallas_call(
        functools.partial(turn_sum_kernel, classes_here, rotations),
        grid=(chunks,),
        in_specs=[
            pl.BlockSpec((local_refs, n), lambda t: (0, 0)),
            pl.BlockSpec((n, width), lambda t: (0, t)),
            pl.BlockSpec((1, width), lambda t: (0, 0)),
        ],
        out_specs=pl.BlockSpec((1, classes_here, width + LANES), lambda t: (t, 0, 0)),
        out_shape=jax.ShapeDtypeStruct((chunks, classes_here, width + LANES), jnp.float32),
        scratch_shapes=[pltpu.VMEM((local_refs, width), jnp.float32)],
        compiler_params=pltpu.CompilerParams(vmem_limit_bytes=60 * 1024 * 1024),
        cost_estimate=pl.CostEstimate(
            flops=2 * local_refs * n * pixels,
            bytes_accessed=2 * local_refs * n + 2 * n * pixels + 4 * classes_here * pixels,
            transcendentals=0,
        ),
    )(by_turn, gathered, angle)


def ring_order(chips):
    if chips == 4:
        return [0, 1, 3, 2]
    order = []
    for row in range(chips // 2):
        order += [2 * row, 2 * row + 1] if row % 2 == 0 else [2 * row + 1, 2 * row]
    return order


def ring_gather(images, n_ref):
    chips = n_ref // 2
    block = images.shape[0]
    ring = ring_order(chips)
    place = {chip: i for i, chip in enumerate(ring)}

    def ahead(chip, hops):
        return ring[(place[chip] + hops) % chips]

    to_next = [(2 * c + k, 2 * ahead(c, 1) + k) for c in range(chips) for k in range(2)]
    to_prev = [(2 * c + k, 2 * ahead(c, -1) + k) for c in range(chips) for k in range(2)]
    to_partner = [(d, d ^ 1) for d in range(n_ref)]
    pieces = [(images, 0, 0, block)]
    from_prev = images
    from_next = images
    for hops in range(1, (chips + 1) // 2):
        from_prev = lax.ppermute(from_prev, "ref", to_next)
        from_next = lax.ppermute(from_next, "ref", to_prev)
        pieces += [(from_prev, -hops, 0, block), (from_next, hops, 0, block)]
    if chips % 2 == 0:
        half = block // 2
        top = lax.ppermute(from_prev[:half], "ref", to_next)
        bottom = lax.ppermute(from_next[half:], "ref", to_prev)
        pieces += [(top, chips // 2, 0, half), (bottom, chips // 2, half, block - half)]
    arrays = [piece[0] for piece in pieces]
    arrays += [lax.ppermute(piece[0], "ref", to_partner) for piece in pieces]
    table = []
    for device in range(n_ref):
        chip, core = device // 2, device % 2
        rows = []
        for side in (core, 1 - core):
            for _, hops, first, count in pieces:
                origin = 2 * ahead(chip, hops) + side
                rows += list(range(origin * block + first, origin * block + first + count))
        table.append(rows)
    return jnp.concatenate(arrays, axis=0), np.array(table, np.int32)


def per_device(chunks, n_ref, images, references, class_prior):
    local_refs, pixels = references.shape
    classes_here = class_prior.shape[0]
    rotations = local_refs // classes_here

    half_norm = 0.5 * jnp.einsum(
        "jp,jp->j", references, references, preferred_element_type=jnp.float32
    )
    offsets = (jnp.log(class_prior)[:, None] - half_norm.reshape(classes_here, rotations)).reshape(
        local_refs
    )
    gathered, table = ring_gather(images, n_ref)
    to_group = jnp.asarray(table)[lax.axis_index("ref")]
    from_group = jnp.asarray(np.argsort(table, axis=1).astype(np.int32))[lax.axis_index("ref")]
    products = lax.dot_general(
        gathered, references, (((1,), (1,)), ((), ())), preferred_element_type=jnp.float32
    )
    scores = products + offsets
    local_max = jnp.max(scores, axis=1)
    local_sum = jnp.sum(jnp.exp(scores - local_max[:, None]), axis=1)
    in_group_order = jnp.take(jnp.stack([local_max, local_sum]), from_group, axis=1)
    stats = lax.all_gather(in_group_order, "ref", axis=0)
    top_score = jnp.max(stats[:, 0], axis=0)
    denominator = jnp.sum(stats[:, 1] * jnp.exp(stats[:, 0] - top_score[None, :]), axis=0)
    norm = jnp.take(jnp.stack([top_score, denominator]), to_group, axis=1)
    top_score, denominator = norm[0], norm[1]
    weights = (jnp.exp(scores - top_score[:, None]) / denominator[:, None]).astype(jnp.bfloat16)

    n = weights.shape[0]
    by_turn = weights.reshape(n, classes_here, rotations).transpose(2, 1, 0).reshape(local_refs, n)
    chunked = turn_and_sum(by_turn, gathered, classes_here, rotations, chunks)
    me = lax.axis_index("img")
    total = lax.dynamic_index_in_dim(chunked, me, 0, keepdims=False)
    for step in range(1, chunks):
        perm = [(src, (src + step) % chunks) for src in range(chunks)]
        outgoing = lax.dynamic_index_in_dim(chunked, (me + step) % chunks, 0, keepdims=False)
        total = total + lax.ppermute(outgoing, "img", perm)
    width = pixels // chunks
    class_sums, class_weights = total[:, :width], total[:, width]
    return (class_sums, class_weights)

def solution(mesh):
    placed = (P(("img", "ref"), None), P("ref", None), P("ref"))
    return jax.shard_map(
        functools.partial(per_device, mesh.shape["img"], mesh.shape["ref"]),
        mesh=mesh,
        in_specs=placed,
        out_specs=(P("ref", "img"), P("ref")),
        check_vma=False,
    )
```

```python
import functools

import jax
import numpy as np
import jax.numpy as jnp
from jax import lax
from jax.experimental import pallas as pl
from jax.experimental.pallas import tpu as pltpu
from jax.sharding import PartitionSpec as P

ANG = 144
LANES = 128
GROUP_COLS = 1152


def turn_sum_kernel(classes_here, rotations, by_turn_ref, images_ref, angle_ref, out_ref, products_ref):
    shift = ANG // rotations
    width = images_ref.shape[1]
    products_ref[...] = jnp.dot(
        by_turn_ref[...], images_ref[...], preferred_element_type=jnp.float32
    )
    rows = 8 if classes_here % 8 == 0 else classes_here
    cols = GROUP_COLS if width % GROUP_COLS == 0 else width
    for row0 in range(0, classes_here, rows):
        for col0 in range(0, width, cols):
            angle = angle_ref[:, col0 : col0 + cols]
            kept = products_ref[row0 : row0 + rows, col0 : col0 + cols]
            every = None
            for turn_index in range(1, rotations):
                start = turn_index * classes_here + row0
                part = products_ref[start : start + rows, col0 : col0 + cols]
                step = turn_index * shift
                ahead = pltpu.roll(part, cols - step, 1)
                kept = kept + jnp.where(angle < ANG - step, ahead, 0.0)
                every = ahead if every is None else every + ahead
            wrapped = every - (kept - products_ref[row0 : row0 + rows, col0 : col0 + cols])
            out_ref[0, row0 : row0 + rows, col0 : col0 + cols] = kept + pltpu.roll(wrapped, ANG, 1)
    mass = jnp.sum(by_turn_ref[...].astype(jnp.float32), axis=1, keepdims=True)
    class_mass = mass[0:classes_here]
    for turn_index in range(1, rotations):
        class_mass = class_mass + mass[turn_index * classes_here : (turn_index + 1) * classes_here]
    out_ref[0, :, width:] = jnp.broadcast_to(class_mass, (classes_here, LANES))


def turn_and_sum(by_turn, gathered, classes_here, rotations, chunks):
    local_refs, n = by_turn.shape
    pixels = gathered.shape[1]
    width = pixels // chunks
    angle = (jnp.arange(width, dtype=jnp.int32) % ANG).reshape(1, width)
    return pl.pallas_call(
        functools.partial(turn_sum_kernel, classes_here, rotations),
        grid=(chunks,),
        in_specs=[
            pl.BlockSpec((local_refs, n), lambda t: (0, 0)),
            pl.BlockSpec((n, width), lambda t: (0, t)),
            pl.BlockSpec((1, width), lambda t: (0, 0)),
        ],
        out_specs=pl.BlockSpec((1, classes_here, width + LANES), lambda t: (t, 0, 0)),
        out_shape=jax.ShapeDtypeStruct((chunks, classes_here, width + LANES), jnp.float32),
        scratch_shapes=[pltpu.VMEM((local_refs, width), jnp.float32)],
        compiler_params=pltpu.CompilerParams(vmem_limit_bytes=60 * 1024 * 1024),
        cost_estimate=pl.CostEstimate(
            flops=2 * local_refs * n * pixels,
            bytes_accessed=2 * local_refs * n + 2 * n * pixels + 4 * classes_here * pixels,
            transcendentals=0,
        ),
    )(by_turn, gathered, angle)


def ring_order(chips):
    if chips == 4:
        return [0, 1, 3, 2]
    order = []
    for row in range(chips // 2):
        order += [2 * row, 2 * row + 1] if row % 2 == 0 else [2 * row + 1, 2 * row]
    return order


def ring_gather(images, n_ref):
    chips = n_ref // 2
    block = images.shape[0]
    ring = ring_order(chips)
    place = {chip: i for i, chip in enumerate(ring)}

    def ahead(chip, hops):
        return ring[(place[chip] + hops) % chips]

    to_next = [(2 * c + k, 2 * ahead(c, 1) + k) for c in range(chips) for k in range(2)]
    to_prev = [(2 * c + k, 2 * ahead(c, -1) + k) for c in range(chips) for k in range(2)]
    to_partner = [(d, d ^ 1) for d in range(n_ref)]
    pieces = [(images, 0, 0, block)]
    from_prev = images
    from_next = images
    for hops in range(1, (chips + 1) // 2):
        from_prev = lax.ppermute(from_prev, "ref", to_next)
        from_next = lax.ppermute(from_next, "ref", to_prev)
        pieces += [(from_prev, -hops, 0, block), (from_next, hops, 0, block)]
    if chips % 2 == 0:
        half = block // 2
        top = lax.ppermute(from_prev[:half], "ref", to_next)
        bottom = lax.ppermute(from_next[half:], "ref", to_prev)
        pieces += [(top, chips // 2, 0, half), (bottom, chips // 2, half, block - half)]
    arrays = [piece[0] for piece in pieces]
    arrays += [lax.ppermute(piece[0], "ref", to_partner) for piece in pieces]
    table = []
    for device in range(n_ref):
        chip, core = device // 2, device % 2
        starts = []
        for side in (core, 1 - core):
            for _, hops, first, _ in pieces:
                starts.append((2 * ahead(chip, hops) + side) * block + first)
        table.append(starts)
    starts = jnp.asarray(np.array(table, np.int32))[lax.axis_index("ref")]
    gathered = jnp.zeros((n_ref * block,) + images.shape[1:], images.dtype)
    for index, array in enumerate(arrays):
        gathered = lax.dynamic_update_slice(gathered, array, (starts[index], 0))
    return gathered


def per_device(chunks, n_ref, images, references, class_prior):
    local_refs, pixels = references.shape
    classes_here = class_prior.shape[0]
    rotations = local_refs // classes_here

    half_norm = 0.5 * jnp.einsum(
        "jp,jp->j", references, references, preferred_element_type=jnp.float32
    )
    offsets = (jnp.log(class_prior)[:, None] - half_norm.reshape(classes_here, rotations)).reshape(
        local_refs
    )
    gathered = ring_gather(images, n_ref)
    products = lax.dot_general(
        gathered, references, (((1,), (1,)), ((), ())), preferred_element_type=jnp.float32
    )
    scores = products + offsets
    local_max = jnp.max(scores, axis=1)
    local_sum = jnp.sum(jnp.exp(scores - local_max[:, None]), axis=1)
    stats = lax.all_gather(jnp.stack([local_max, local_sum]), "ref", axis=0)
    top_score = jnp.max(stats[:, 0], axis=0)
    denominator = jnp.sum(stats[:, 1] * jnp.exp(stats[:, 0] - top_score[None, :]), axis=0)
    weights = (jnp.exp(scores - top_score[:, None]) / denominator[:, None]).astype(jnp.bfloat16)

    n = weights.shape[0]
    by_turn = weights.reshape(n, classes_here, rotations).transpose(2, 1, 0).reshape(local_refs, n)
    chunked = turn_and_sum(by_turn, gathered, classes_here, rotations, chunks)
    me = lax.axis_index("img")
    total = lax.dynamic_index_in_dim(chunked, me, 0, keepdims=False)
    for step in range(1, chunks):
        perm = [(src, (src + step) % chunks) for src in range(chunks)]
        outgoing = lax.dynamic_index_in_dim(chunked, (me + step) % chunks, 0, keepdims=False)
        total = total + lax.ppermute(outgoing, "img", perm)
    width = pixels // chunks
    class_sums, class_weights = total[:, :width], total[:, width]
    return (class_sums, class_weights)

def solution(mesh):
    placed = (P(("img", "ref"), None), P("ref", None), P("ref"))
    return jax.shard_map(
        functools.partial(per_device, mesh.shape["img"], mesh.shape["ref"]),
        mesh=mesh,
        in_specs=placed,
        out_specs=(P("ref", "img"), P("ref")),
        check_vma=False,
    )
```

```python
import functools

import jax
import numpy as np
import jax.numpy as jnp
from jax import lax
from jax.experimental import pallas as pl
from jax.experimental.pallas import tpu as pltpu
from jax.sharding import PartitionSpec as P

ANG = 144
LANES = 128
GROUP_COLS = 1152


def turn_sum_kernel(
    classes_here, rotations, by_turn_ref, early_ref, late_ref, angle_ref, out_ref, products_ref
):
    shift = ANG // rotations
    width = early_ref.shape[1]
    split = early_ref.shape[0]
    products_ref[...] = jnp.dot(
        by_turn_ref[:, :split], early_ref[...], preferred_element_type=jnp.float32
    ) + jnp.dot(by_turn_ref[:, split:], late_ref[...], preferred_element_type=jnp.float32)
    rows = 8 if classes_here % 8 == 0 else classes_here
    cols = GROUP_COLS if width % GROUP_COLS == 0 else width
    for row0 in range(0, classes_here, rows):
        for col0 in range(0, width, cols):
            angle = angle_ref[:, col0 : col0 + cols]
            kept = products_ref[row0 : row0 + rows, col0 : col0 + cols]
            every = None
            for turn_index in range(1, rotations):
                start = turn_index * classes_here + row0
                part = products_ref[start : start + rows, col0 : col0 + cols]
                step = turn_index * shift
                ahead = pltpu.roll(part, cols - step, 1)
                kept = kept + jnp.where(angle < ANG - step, ahead, 0.0)
                every = ahead if every is None else every + ahead
            wrapped = every - (kept - products_ref[row0 : row0 + rows, col0 : col0 + cols])
            out_ref[0, row0 : row0 + rows, col0 : col0 + cols] = kept + pltpu.roll(wrapped, ANG, 1)
    mass = jnp.sum(by_turn_ref[...].astype(jnp.float32), axis=1, keepdims=True)
    class_mass = mass[0:classes_here]
    for turn_index in range(1, rotations):
        class_mass = class_mass + mass[turn_index * classes_here : (turn_index + 1) * classes_here]
    out_ref[0, :, width:] = jnp.broadcast_to(class_mass, (classes_here, LANES))


def turn_and_sum(by_turn, early, late, classes_here, rotations, chunks):
    local_refs, n = by_turn.shape
    pixels = early.shape[1]
    width = pixels // chunks
    angle = (jnp.arange(width, dtype=jnp.int32) % ANG).reshape(1, width)
    return pl.pallas_call(
        functools.partial(turn_sum_kernel, classes_here, rotations),
        grid=(chunks,),
        in_specs=[
            pl.BlockSpec((local_refs, n), lambda t: (0, 0)),
            pl.BlockSpec((early.shape[0], width), lambda t: (0, t)),
            pl.BlockSpec((late.shape[0], width), lambda t: (0, t)),
            pl.BlockSpec((1, width), lambda t: (0, 0)),
        ],
        out_specs=pl.BlockSpec((1, classes_here, width + LANES), lambda t: (t, 0, 0)),
        out_shape=jax.ShapeDtypeStruct((chunks, classes_here, width + LANES), jnp.float32),
        scratch_shapes=[pltpu.VMEM((local_refs, width), jnp.float32)],
        compiler_params=pltpu.CompilerParams(vmem_limit_bytes=60 * 1024 * 1024),
        cost_estimate=pl.CostEstimate(
            flops=2 * local_refs * n * pixels,
            bytes_accessed=2 * local_refs * n + 2 * n * pixels + 4 * classes_here * pixels,
            transcendentals=0,
        ),
    )(by_turn, early, late, angle)


def ring_order(chips):
    if chips == 4:
        return [0, 1, 3, 2]
    order = []
    for row in range(chips // 2):
        order += [2 * row, 2 * row + 1] if row % 2 == 0 else [2 * row + 1, 2 * row]
    return order


def ring_gather(images, n_ref):
    chips = n_ref // 2
    block = images.shape[0]
    ring = ring_order(chips)
    place = {chip: i for i, chip in enumerate(ring)}

    def ahead(chip, hops):
        return ring[(place[chip] + hops) % chips]

    to_next = [(2 * c + k, 2 * ahead(c, 1) + k) for c in range(chips) for k in range(2)]
    to_prev = [(2 * c + k, 2 * ahead(c, -1) + k) for c in range(chips) for k in range(2)]
    to_partner = [(d, d ^ 1) for d in range(n_ref)]
    pieces = [(images, 0, 0, block)]
    from_prev = images
    from_next = images
    for hops in range(1, (chips + 1) // 2):
        from_prev = lax.ppermute(from_prev, "ref", to_next)
        from_next = lax.ppermute(from_next, "ref", to_prev)
        pieces += [(from_prev, -hops, 0, block), (from_next, hops, 0, block)]
    if chips % 2 == 0:
        half = block // 2
        top = lax.ppermute(from_prev[:half], "ref", to_next)
        bottom = lax.ppermute(from_next[half:], "ref", to_prev)
        pieces += [(top, chips // 2, 0, half), (bottom, chips // 2, half, block - half)]
    partner_pieces = [(lax.ppermute(piece[0], "ref", to_partner),) + piece[1:] for piece in pieces]
    full = [piece for piece in pieces if piece[3] == block]
    early = full + partner_pieces[:1]
    late = [piece for piece in pieces if piece[3] != block] + partner_pieces[1:]
    table = []
    for device in range(n_ref):
        chip, core = device // 2, device % 2
        rows = []
        for group in (early, late):
            for index, (_, hops, first, count) in enumerate(group):
                side = 1 - core if any(group[index] is p for p in partner_pieces) else core
                origin = 2 * ahead(chip, hops) + side
                rows += list(range(origin * block + first, origin * block + first + count))
        table.append(rows)
    return (
        jnp.concatenate([piece[0] for piece in early], axis=0),
        jnp.concatenate([piece[0] for piece in late], axis=0),
        np.array(table, np.int32),
    )


def per_device(chunks, n_ref, images, references, class_prior):
    local_refs, pixels = references.shape
    classes_here = class_prior.shape[0]
    rotations = local_refs // classes_here

    half_norm = 0.5 * jnp.einsum(
        "jp,jp->j", references, references, preferred_element_type=jnp.float32
    )
    offsets = (jnp.log(class_prior)[:, None] - half_norm.reshape(classes_here, rotations)).reshape(
        local_refs
    )
    early, late, table = ring_gather(images, n_ref)
    to_group = jnp.asarray(table)[lax.axis_index("ref")]
    from_group = jnp.asarray(np.argsort(table, axis=1).astype(np.int32))[lax.axis_index("ref")]
    scores = jnp.concatenate(
        [
            lax.dot_general(
                group, references, (((1,), (1,)), ((), ())), preferred_element_type=jnp.float32
            )
            for group in (early, late)
        ],
        axis=0,
    ) + offsets
    local_max = jnp.max(scores, axis=1)
    local_sum = jnp.sum(jnp.exp(scores - local_max[:, None]), axis=1)
    in_group_order = jnp.take(jnp.stack([local_max, local_sum]), from_group, axis=1)
    stats = lax.all_gather(in_group_order, "ref", axis=0)
    top_score = jnp.max(stats[:, 0], axis=0)
    denominator = jnp.sum(stats[:, 1] * jnp.exp(stats[:, 0] - top_score[None, :]), axis=0)
    norm = jnp.take(jnp.stack([top_score, denominator]), to_group, axis=1)
    top_score, denominator = norm[0], norm[1]
    weights = (jnp.exp(scores - top_score[:, None]) / denominator[:, None]).astype(jnp.bfloat16)

    n = weights.shape[0]
    by_turn = weights.reshape(n, classes_here, rotations).transpose(2, 1, 0).reshape(local_refs, n)
    chunked = turn_and_sum(by_turn, early, late, classes_here, rotations, chunks)
    me = lax.axis_index("img")
    total = lax.dynamic_index_in_dim(chunked, me, 0, keepdims=False)
    for step in range(1, chunks):
        perm = [(src, (src + step) % chunks) for src in range(chunks)]
        outgoing = lax.dynamic_index_in_dim(chunked, (me + step) % chunks, 0, keepdims=False)
        total = total + lax.ppermute(outgoing, "img", perm)
    width = pixels // chunks
    class_sums, class_weights = total[:, :width], total[:, width]
    return (class_sums, class_weights)

def solution(mesh):
    placed = (P(("img", "ref"), None), P("ref", None), P("ref"))
    return jax.shard_map(
        functools.partial(per_device, mesh.shape["img"], mesh.shape["ref"]),
        mesh=mesh,
        in_specs=placed,
        out_specs=(P("ref", "img"), P("ref")),
        check_vma=False,
    )
```

```python
import functools

import jax
import numpy as np
import jax.numpy as jnp
from jax import lax
from jax.experimental import pallas as pl
from jax.experimental.pallas import tpu as pltpu
from jax.sharding import PartitionSpec as P

ANG = 144
LANES = 128
GROUP_COLS = 1152


def turn_sum_kernel(
    classes_here, rotations, me_ref, by_turn_ref, images_ref, angle_ref, out_ref, products_ref
):
    shift = ANG // rotations
    width = images_ref.shape[1]
    products_ref[...] = jnp.dot(
        by_turn_ref[...], images_ref[...], preferred_element_type=jnp.float32
    )
    rows = 8 if classes_here % 8 == 0 else classes_here
    cols = GROUP_COLS if width % GROUP_COLS == 0 else width
    for row0 in range(0, classes_here, rows):
        for col0 in range(0, width, cols):
            angle = angle_ref[:, col0 : col0 + cols]
            kept = products_ref[row0 : row0 + rows, col0 : col0 + cols]
            every = None
            for turn_index in range(1, rotations):
                start = turn_index * classes_here + row0
                part = products_ref[start : start + rows, col0 : col0 + cols]
                step = turn_index * shift
                ahead = pltpu.roll(part, cols - step, 1)
                kept = kept + jnp.where(angle < ANG - step, ahead, 0.0)
                every = ahead if every is None else every + ahead
            wrapped = every - (kept - products_ref[row0 : row0 + rows, col0 : col0 + cols])
            out_ref[0, row0 : row0 + rows, col0 : col0 + cols] = kept + pltpu.roll(wrapped, ANG, 1)
    mass = jnp.sum(by_turn_ref[...].astype(jnp.float32), axis=1, keepdims=True)
    class_mass = mass[0:classes_here]
    for turn_index in range(1, rotations):
        class_mass = class_mass + mass[turn_index * classes_here : (turn_index + 1) * classes_here]
    out_ref[0, :, width:] = jnp.broadcast_to(class_mass, (classes_here, LANES))


def turn_and_sum(by_turn, gathered, classes_here, rotations, chunks, me, first, count):
    local_refs, n = by_turn.shape
    pixels = gathered.shape[1]
    width = pixels // chunks
    angle = (jnp.arange(width, dtype=jnp.int32) % ANG).reshape(1, width)

    def chunk_of(t, me_ref):
        return (0, (me_ref[0] + first + t) % chunks)

    return pl.pallas_call(
        functools.partial(turn_sum_kernel, classes_here, rotations),
        grid_spec=pltpu.PrefetchScalarGridSpec(
            num_scalar_prefetch=1,
            grid=(count,),
            in_specs=[
                pl.BlockSpec((local_refs, n), lambda t, me_ref: (0, 0)),
                pl.BlockSpec((n, width), chunk_of),
                pl.BlockSpec((1, width), lambda t, me_ref: (0, 0)),
            ],
            out_specs=pl.BlockSpec((1, classes_here, width + LANES), lambda t, me_ref: (t, 0, 0)),
            scratch_shapes=[pltpu.VMEM((local_refs, width), jnp.float32)],
        ),
        out_shape=jax.ShapeDtypeStruct((count, classes_here, width + LANES), jnp.float32),
        compiler_params=pltpu.CompilerParams(vmem_limit_bytes=60 * 1024 * 1024),
        cost_estimate=pl.CostEstimate(
            flops=2 * local_refs * n * width * count,
            bytes_accessed=2 * local_refs * n + 2 * n * width * count + 4 * classes_here * width * count,
            transcendentals=0,
        ),
    )(jnp.reshape(me, (1,)).astype(jnp.int32), by_turn, gathered, angle)

def ring_order(chips):
    if chips == 4:
        return [0, 1, 3, 2]
    order = []
    for row in range(chips // 2):
        order += [2 * row, 2 * row + 1] if row % 2 == 0 else [2 * row + 1, 2 * row]
    return order


def ring_gather(images, n_ref):
    chips = n_ref // 2
    block = images.shape[0]
    ring = ring_order(chips)
    place = {chip: i for i, chip in enumerate(ring)}

    def ahead(chip, hops):
        return ring[(place[chip] + hops) % chips]

    to_next = [(2 * c + k, 2 * ahead(c, 1) + k) for c in range(chips) for k in range(2)]
    to_prev = [(2 * c + k, 2 * ahead(c, -1) + k) for c in range(chips) for k in range(2)]
    to_partner = [(d, d ^ 1) for d in range(n_ref)]
    pieces = [(images, 0, 0, block)]
    from_prev = images
    from_next = images
    for hops in range(1, (chips + 1) // 2):
        from_prev = lax.ppermute(from_prev, "ref", to_next)
        from_next = lax.ppermute(from_next, "ref", to_prev)
        pieces += [(from_prev, -hops, 0, block), (from_next, hops, 0, block)]
    if chips % 2 == 0:
        half = block // 2
        top = lax.ppermute(from_prev[:half], "ref", to_next)
        bottom = lax.ppermute(from_next[half:], "ref", to_prev)
        pieces += [(top, chips // 2, 0, half), (bottom, chips // 2, half, block - half)]
    arrays = [piece[0] for piece in pieces]
    arrays += [lax.ppermute(piece[0], "ref", to_partner) for piece in pieces]
    table = []
    for device in range(n_ref):
        chip, core = device // 2, device % 2
        rows = []
        for side in (core, 1 - core):
            for _, hops, first, count in pieces:
                origin = 2 * ahead(chip, hops) + side
                rows += list(range(origin * block + first, origin * block + first + count))
        table.append(rows)
    return jnp.concatenate(arrays, axis=0), np.array(table, np.int32)


def per_device(chunks, n_ref, images, references, class_prior):
    local_refs, pixels = references.shape
    classes_here = class_prior.shape[0]
    rotations = local_refs // classes_here

    half_norm = 0.5 * jnp.einsum(
        "jp,jp->j", references, references, preferred_element_type=jnp.float32
    )
    offsets = (jnp.log(class_prior)[:, None] - half_norm.reshape(classes_here, rotations)).reshape(
        local_refs
    )
    gathered, table = ring_gather(images, n_ref)
    to_group = jnp.asarray(table)[lax.axis_index("ref")]
    from_group = jnp.asarray(np.argsort(table, axis=1).astype(np.int32))[lax.axis_index("ref")]
    products = lax.dot_general(
        gathered, references, (((1,), (1,)), ((), ())), preferred_element_type=jnp.float32
    )
    scores = products + offsets
    local_max = jnp.max(scores, axis=1)
    local_sum = jnp.sum(jnp.exp(scores - local_max[:, None]), axis=1)
    in_group_order = jnp.take(jnp.stack([local_max, local_sum]), from_group, axis=1)
    stats = lax.all_gather(in_group_order, "ref", axis=0)
    top_score = jnp.max(stats[:, 0], axis=0)
    denominator = jnp.sum(stats[:, 1] * jnp.exp(stats[:, 0] - top_score[None, :]), axis=0)
    norm = jnp.take(jnp.stack([top_score, denominator]), to_group, axis=1)
    top_score, denominator = norm[0], norm[1]
    weights = (jnp.exp(scores - top_score[:, None]) / denominator[:, None]).astype(jnp.bfloat16)

    n = weights.shape[0]
    by_turn = weights.reshape(n, classes_here, rotations).transpose(2, 1, 0).reshape(local_refs, n)
    me = lax.axis_index("img")
    received = []
    if chunks > 1:
        outgoing = turn_and_sum(by_turn, gathered, classes_here, rotations, chunks, me, 1, chunks - 1)
        received = [
            lax.ppermute(outgoing[step - 1], "img", [(src, (src + step) % chunks) for src in range(chunks)])
            for step in range(1, chunks)
        ]
    total = turn_and_sum(by_turn, gathered, classes_here, rotations, chunks, me, 0, 1)[0]
    for part in received:
        total = total + part
    width = pixels // chunks
    class_sums, class_weights = total[:, :width], total[:, width]
    return (class_sums, class_weights)

def solution(mesh):
    placed = (P(("img", "ref"), None), P("ref", None), P("ref"))
    return jax.shard_map(
        functools.partial(per_device, mesh.shape["img"], mesh.shape["ref"]),
        mesh=mesh,
        in_specs=placed,
        out_specs=(P("ref", "img"), P("ref")),
        check_vma=False,
    )
```

```python
import functools

import jax
import numpy as np
import jax.numpy as jnp
from jax import lax
from jax.experimental import pallas as pl
from jax.experimental.pallas import tpu as pltpu
from jax.sharding import PartitionSpec as P

ANG = 144
LANES = 128
GROUP_COLS = 1152


def turn_sum_kernel(classes_here, rotations, count, me_ref, by_turn_ref, images_ref, angle_ref, *rest):
    out_refs, products_ref, out_ref = rest[:count], rest[count], rest[count + 1]
    shift = ANG // rotations
    width = images_ref.shape[1]
    products_ref[...] = jnp.dot(
        by_turn_ref[...], images_ref[...], preferred_element_type=jnp.float32
    )
    rows = 8 if classes_here % 8 == 0 else classes_here
    cols = GROUP_COLS if width % GROUP_COLS == 0 else width
    for row0 in range(0, classes_here, rows):
        for col0 in range(0, width, cols):
            angle = angle_ref[:, col0 : col0 + cols]
            kept = products_ref[row0 : row0 + rows, col0 : col0 + cols]
            every = None
            for turn_index in range(1, rotations):
                start = turn_index * classes_here + row0
                part = products_ref[start : start + rows, col0 : col0 + cols]
                step = turn_index * shift
                ahead = pltpu.roll(part, cols - step, 1)
                kept = kept + jnp.where(angle < ANG - step, ahead, 0.0)
                every = ahead if every is None else every + ahead
            wrapped = every - (kept - products_ref[row0 : row0 + rows, col0 : col0 + cols])
            out_ref[row0 : row0 + rows, col0 : col0 + cols] = kept + pltpu.roll(wrapped, ANG, 1)
    mass = jnp.sum(by_turn_ref[...].astype(jnp.float32), axis=1, keepdims=True)
    class_mass = mass[0:classes_here]
    for turn_index in range(1, rotations):
        class_mass = class_mass + mass[turn_index * classes_here : (turn_index + 1) * classes_here]
    out_ref[:, width:] = jnp.broadcast_to(class_mass, (classes_here, LANES))
    step = pl.program_id(0)
    for index, target in enumerate(out_refs):

        @pl.when(step == index)
        def _():
            target[...] = out_ref[...]


def turn_and_sum(by_turn, gathered, classes_here, rotations, chunks, me, first, count):
    local_refs, n = by_turn.shape
    pixels = gathered.shape[1]
    width = pixels // chunks
    angle = (jnp.arange(width, dtype=jnp.int32) % ANG).reshape(1, width)

    def chunk_of(t, me_ref):
        return (0, (me_ref[0] + first + t) % chunks)

    return pl.pallas_call(
        functools.partial(turn_sum_kernel, classes_here, rotations, count),
        grid_spec=pltpu.PrefetchScalarGridSpec(
            num_scalar_prefetch=1,
            grid=(count,),
            in_specs=[
                pl.BlockSpec((local_refs, n), lambda t, me_ref: (0, 0)),
                pl.BlockSpec((n, width), chunk_of),
                pl.BlockSpec((1, width), lambda t, me_ref: (0, 0)),
            ],
            out_specs=[
                pl.BlockSpec((classes_here, width + LANES), lambda t, me_ref: (0, 0))
                for _ in range(count)
            ],
            scratch_shapes=[
                pltpu.VMEM((local_refs, width), jnp.float32),
                pltpu.VMEM((classes_here, width + LANES), jnp.float32),
            ],
        ),
        out_shape=[
            jax.ShapeDtypeStruct((classes_here, width + LANES), jnp.float32) for _ in range(count)
        ],
        compiler_params=pltpu.CompilerParams(vmem_limit_bytes=60 * 1024 * 1024),
        cost_estimate=pl.CostEstimate(
            flops=2 * local_refs * n * width * count,
            bytes_accessed=2 * local_refs * n + 2 * n * width * count + 4 * classes_here * width * count,
            transcendentals=0,
        ),
    )(jnp.reshape(me, (1,)).astype(jnp.int32), by_turn, gathered, angle)

def ring_order(chips):
    if chips == 4:
        return [0, 1, 3, 2]
    order = []
    for row in range(chips // 2):
        order += [2 * row, 2 * row + 1] if row % 2 == 0 else [2 * row + 1, 2 * row]
    return order


def ring_gather(images, n_ref):
    chips = n_ref // 2
    block = images.shape[0]
    ring = ring_order(chips)
    place = {chip: i for i, chip in enumerate(ring)}

    def ahead(chip, hops):
        return ring[(place[chip] + hops) % chips]

    to_next = [(2 * c + k, 2 * ahead(c, 1) + k) for c in range(chips) for k in range(2)]
    to_prev = [(2 * c + k, 2 * ahead(c, -1) + k) for c in range(chips) for k in range(2)]
    to_partner = [(d, d ^ 1) for d in range(n_ref)]
    pieces = [(images, 0, 0, block)]
    from_prev = images
    from_next = images
    for hops in range(1, (chips + 1) // 2):
        from_prev = lax.ppermute(from_prev, "ref", to_next)
        from_next = lax.ppermute(from_next, "ref", to_prev)
        pieces += [(from_prev, -hops, 0, block), (from_next, hops, 0, block)]
    if chips % 2 == 0:
        half = block // 2
        top = lax.ppermute(from_prev[:half], "ref", to_next)
        bottom = lax.ppermute(from_next[half:], "ref", to_prev)
        pieces += [(top, chips // 2, 0, half), (bottom, chips // 2, half, block - half)]
    arrays = [piece[0] for piece in pieces]
    arrays += [lax.ppermute(piece[0], "ref", to_partner) for piece in pieces]
    table = []
    for device in range(n_ref):
        chip, core = device // 2, device % 2
        rows = []
        for side in (core, 1 - core):
            for _, hops, first, count in pieces:
                origin = 2 * ahead(chip, hops) + side
                rows += list(range(origin * block + first, origin * block + first + count))
        table.append(rows)
    return jnp.concatenate(arrays, axis=0), np.array(table, np.int32)


def per_device(chunks, n_ref, images, references, class_prior):
    local_refs, pixels = references.shape
    classes_here = class_prior.shape[0]
    rotations = local_refs // classes_here

    half_norm = 0.5 * jnp.einsum(
        "jp,jp->j", references, references, preferred_element_type=jnp.float32
    )
    offsets = (jnp.log(class_prior)[:, None] - half_norm.reshape(classes_here, rotations)).reshape(
        local_refs
    )
    gathered, table = ring_gather(images, n_ref)
    to_group = jnp.asarray(table)[lax.axis_index("ref")]
    from_group = jnp.asarray(np.argsort(table, axis=1).astype(np.int32))[lax.axis_index("ref")]
    products = lax.dot_general(
        gathered, references, (((1,), (1,)), ((), ())), preferred_element_type=jnp.float32
    )
    scores = products + offsets
    local_max = jnp.max(scores, axis=1)
    local_sum = jnp.sum(jnp.exp(scores - local_max[:, None]), axis=1)
    in_group_order = jnp.take(jnp.stack([local_max, local_sum]), from_group, axis=1)
    stats = lax.all_gather(in_group_order, "ref", axis=0)
    top_score = jnp.max(stats[:, 0], axis=0)
    denominator = jnp.sum(stats[:, 1] * jnp.exp(stats[:, 0] - top_score[None, :]), axis=0)
    norm = jnp.take(jnp.stack([top_score, denominator]), to_group, axis=1)
    top_score, denominator = norm[0], norm[1]
    weights = (jnp.exp(scores - top_score[:, None]) / denominator[:, None]).astype(jnp.bfloat16)

    n = weights.shape[0]
    by_turn = weights.reshape(n, classes_here, rotations).transpose(2, 1, 0).reshape(local_refs, n)
    me = lax.axis_index("img")
    received = []
    if chunks > 1:
        outgoing = turn_and_sum(by_turn, gathered, classes_here, rotations, chunks, me, 1, chunks - 1)
        received = [
            lax.ppermute(outgoing[step - 1], "img", [(src, (src + step) % chunks) for src in range(chunks)])
            for step in range(1, chunks)
        ]
    total = turn_and_sum(by_turn, gathered, classes_here, rotations, chunks, me, 0, 1)[0]
    for part in received:
        total = total + part
    width = pixels // chunks
    class_sums, class_weights = total[:, :width], total[:, width]
    return (class_sums, class_weights)

def solution(mesh):
    placed = (P(("img", "ref"), None), P("ref", None), P("ref"))
    return jax.shard_map(
        functools.partial(per_device, mesh.shape["img"], mesh.shape["ref"]),
        mesh=mesh,
        in_specs=placed,
        out_specs=(P("ref", "img"), P("ref")),
        check_vma=False,
    )
```

```python
import functools

import jax
import numpy as np
import jax.numpy as jnp
from jax import lax
from jax.experimental import pallas as pl
from jax.experimental.pallas import tpu as pltpu
from jax.sharding import PartitionSpec as P

ANG = 144
LANES = 128
GROUP_COLS = 1152


def turn_sum_kernel(classes_here, rotations, count, me_ref, by_turn_ref, images_ref, angle_ref, *rest):
    out_refs, products_ref, out_ref = rest[:count], rest[count], rest[count + 1]
    shift = ANG // rotations
    width = images_ref.shape[1]
    products_ref[...] = jnp.dot(
        by_turn_ref[...], images_ref[...], preferred_element_type=jnp.float32
    )
    rows = 8 if classes_here % 8 == 0 else classes_here
    cols = GROUP_COLS if width % GROUP_COLS == 0 else width
    for row0 in range(0, classes_here, rows):
        for col0 in range(0, width, cols):
            angle = angle_ref[:, col0 : col0 + cols]
            kept = products_ref[row0 : row0 + rows, col0 : col0 + cols]
            every = None
            for turn_index in range(1, rotations):
                start = turn_index * classes_here + row0
                part = products_ref[start : start + rows, col0 : col0 + cols]
                step = turn_index * shift
                ahead = pltpu.roll(part, cols - step, 1)
                kept = kept + jnp.where(angle < ANG - step, ahead, 0.0)
                every = ahead if every is None else every + ahead
            wrapped = every - (kept - products_ref[row0 : row0 + rows, col0 : col0 + cols])
            out_ref[row0 : row0 + rows, col0 : col0 + cols] = kept + pltpu.roll(wrapped, ANG, 1)
    mass = jnp.sum(by_turn_ref[...].astype(jnp.float32), axis=1, keepdims=True)
    class_mass = mass[0:classes_here]
    for turn_index in range(1, rotations):
        class_mass = class_mass + mass[turn_index * classes_here : (turn_index + 1) * classes_here]
    out_ref[:, width:] = jnp.broadcast_to(class_mass, (classes_here, LANES))
    step = pl.program_id(0)
    for index, target in enumerate(out_refs):

        @pl.when(step == index)
        def _():
            target[...] = out_ref[...]


def turn_and_sum(by_turn, gathered, classes_here, rotations, chunks, me, first, count):
    local_refs, n = by_turn.shape
    pixels = gathered.shape[1]
    width = pixels // chunks
    angle = (jnp.arange(width, dtype=jnp.int32) % ANG).reshape(1, width)

    def chunk_of(t, me_ref):
        return (0, (me_ref[0] + first + t) % chunks)

    return pl.pallas_call(
        functools.partial(turn_sum_kernel, classes_here, rotations, count),
        grid_spec=pltpu.PrefetchScalarGridSpec(
            num_scalar_prefetch=1,
            grid=(count,),
            in_specs=[
                pl.BlockSpec((local_refs, n), lambda t, me_ref: (0, 0)),
                pl.BlockSpec((n, width), chunk_of),
                pl.BlockSpec((1, width), lambda t, me_ref: (0, 0)),
            ],
            out_specs=[
                pl.BlockSpec((classes_here, width + LANES), lambda t, me_ref: (0, 0))
                for _ in range(count)
            ],
            scratch_shapes=[
                pltpu.VMEM((local_refs, width), jnp.float32),
                pltpu.VMEM((classes_here, width + LANES), jnp.float32),
            ],
        ),
        out_shape=[
            jax.ShapeDtypeStruct((classes_here, width + LANES), jnp.float32) for _ in range(count)
        ],
        compiler_params=pltpu.CompilerParams(vmem_limit_bytes=60 * 1024 * 1024),
        cost_estimate=pl.CostEstimate(
            flops=2 * local_refs * n * width * count,
            bytes_accessed=2 * local_refs * n + 2 * n * width * count + 4 * classes_here * width * count,
            transcendentals=0,
        ),
    )(jnp.reshape(me, (1,)).astype(jnp.int32), by_turn, gathered, angle)

def ring_order(chips):
    if chips == 4:
        return [0, 1, 3, 2]
    order = []
    for row in range(chips // 2):
        order += [2 * row, 2 * row + 1] if row % 2 == 0 else [2 * row + 1, 2 * row]
    return order


def ring_gather(images, n_ref):
    chips = n_ref // 2
    block = images.shape[0]
    ring = ring_order(chips)
    place = {chip: i for i, chip in enumerate(ring)}

    def ahead(chip, hops):
        return ring[(place[chip] + hops) % chips]

    to_next = [(2 * c + k, 2 * ahead(c, 1) + k) for c in range(chips) for k in range(2)]
    to_prev = [(2 * c + k, 2 * ahead(c, -1) + k) for c in range(chips) for k in range(2)]
    to_partner = [(d, d ^ 1) for d in range(n_ref)]
    pieces = [(images, 0, 0, block)]
    from_prev = images
    from_next = images
    for hops in range(1, (chips + 1) // 2):
        from_prev = lax.ppermute(from_prev, "ref", to_next)
        from_next = lax.ppermute(from_next, "ref", to_prev)
        pieces += [(from_prev, -hops, 0, block), (from_next, hops, 0, block)]
    if chips % 2 == 0:
        half = block // 2
        top = lax.ppermute(from_prev[:half], "ref", to_next)
        bottom = lax.ppermute(from_next[half:], "ref", to_prev)
        pieces += [(top, chips // 2, 0, half), (bottom, chips // 2, half, block - half)]
    arrays = [piece[0] for piece in pieces]
    arrays += [lax.ppermute(piece[0], "ref", to_partner) for piece in pieces]
    table = []
    for device in range(n_ref):
        chip, core = device // 2, device % 2
        rows = []
        for side in (core, 1 - core):
            for _, hops, first, count in pieces:
                origin = 2 * ahead(chip, hops) + side
                rows += list(range(origin * block + first, origin * block + first + count))
        table.append(rows)
    return jnp.concatenate(arrays, axis=0), np.array(table, np.int32)


def per_device(chunks, n_ref, images, references, class_prior):
    local_refs, pixels = references.shape
    classes_here = class_prior.shape[0]
    rotations = local_refs // classes_here

    half_norm = 0.5 * jnp.einsum(
        "jp,jp->j", references, references, preferred_element_type=jnp.float32
    )
    offsets = (jnp.log(class_prior)[:, None] - half_norm.reshape(classes_here, rotations)).reshape(
        local_refs
    )
    gathered, table = ring_gather(images, n_ref)
    where = np.argsort(table, axis=1)
    same_image = np.stack([where[:, table[device]] for device in range(n_ref)]).astype(np.int32)
    peer_rows = jnp.asarray(same_image)[lax.axis_index("ref")]
    products = lax.dot_general(
        gathered, references, (((1,), (1,)), ((), ())), preferred_element_type=jnp.float32
    )
    scores = products + offsets
    local_max = jnp.max(scores, axis=1)
    local_sum = jnp.sum(jnp.exp(scores - local_max[:, None]), axis=1)
    stats = lax.all_gather(jnp.stack([local_max, local_sum]), "ref", axis=0)
    stats = jnp.take_along_axis(stats, jnp.broadcast_to(peer_rows[:, None, :], stats.shape), axis=2)
    top_score = jnp.max(stats[:, 0], axis=0)
    denominator = jnp.sum(stats[:, 1] * jnp.exp(stats[:, 0] - top_score[None, :]), axis=0)
    weights = (jnp.exp(scores - top_score[:, None]) / denominator[:, None]).astype(jnp.bfloat16)

    n = weights.shape[0]
    by_turn = weights.reshape(n, classes_here, rotations).transpose(2, 1, 0).reshape(local_refs, n)
    me = lax.axis_index("img")
    received = []
    if chunks > 1:
        outgoing = turn_and_sum(by_turn, gathered, classes_here, rotations, chunks, me, 1, chunks - 1)
        received = [
            lax.ppermute(outgoing[step - 1], "img", [(src, (src + step) % chunks) for src in range(chunks)])
            for step in range(1, chunks)
        ]
    total = turn_and_sum(by_turn, gathered, classes_here, rotations, chunks, me, 0, 1)[0]
    for part in received:
        total = total + part
    width = pixels // chunks
    class_sums, class_weights = total[:, :width], total[:, width]
    return (class_sums, class_weights)

def solution(mesh):
    placed = (P(("img", "ref"), None), P("ref", None), P("ref"))
    return jax.shard_map(
        functools.partial(per_device, mesh.shape["img"], mesh.shape["ref"]),
        mesh=mesh,
        in_specs=placed,
        out_specs=(P("ref", "img"), P("ref")),
        check_vma=False,
    )
```

```python
import functools

import jax
import numpy as np
import jax.numpy as jnp
from jax import lax
from jax.experimental import pallas as pl
from jax.experimental.pallas import tpu as pltpu
from jax.sharding import PartitionSpec as P

ANG = 144
LANES = 128
GROUP_COLS = 1152


def turn_sum_kernel(classes_here, rotations, count, me_ref, by_turn_ref, images_ref, angle_ref, *rest):
    out_refs, products_ref, out_ref = rest[:count], rest[count], rest[count + 1]
    shift = ANG // rotations
    width = images_ref.shape[1]
    products_ref[...] = jnp.dot(
        by_turn_ref[...], images_ref[...], preferred_element_type=jnp.float32
    )
    rows = 8 if classes_here % 8 == 0 else classes_here
    cols = GROUP_COLS if width % GROUP_COLS == 0 else width
    for row0 in range(0, classes_here, rows):
        for col0 in range(0, width, cols):
            angle = angle_ref[:, col0 : col0 + cols]
            kept = products_ref[row0 : row0 + rows, col0 : col0 + cols]
            every = None
            for turn_index in range(1, rotations):
                start = turn_index * classes_here + row0
                part = products_ref[start : start + rows, col0 : col0 + cols]
                step = turn_index * shift
                ahead = pltpu.roll(part, cols - step, 1)
                kept = kept + jnp.where(angle < ANG - step, ahead, 0.0)
                every = ahead if every is None else every + ahead
            wrapped = every - (kept - products_ref[row0 : row0 + rows, col0 : col0 + cols])
            out_ref[row0 : row0 + rows, col0 : col0 + cols] = kept + pltpu.roll(wrapped, ANG, 1)
    mass = jnp.sum(by_turn_ref[...].astype(jnp.float32), axis=1, keepdims=True)
    class_mass = mass[0:classes_here]
    for turn_index in range(1, rotations):
        class_mass = class_mass + mass[turn_index * classes_here : (turn_index + 1) * classes_here]
    out_ref[:, width:] = jnp.broadcast_to(class_mass, (classes_here, LANES))
    step = pl.program_id(0)
    for index, target in enumerate(out_refs):

        @pl.when(step == index)
        def _():
            target[...] = out_ref[...]


def turn_and_sum(by_turn, gathered, classes_here, rotations, chunks, me, first, count):
    local_refs, n = by_turn.shape
    pixels = gathered.shape[1]
    width = pixels // chunks
    angle = (jnp.arange(width, dtype=jnp.int32) % ANG).reshape(1, width)

    def chunk_of(t, me_ref):
        return (0, (me_ref[0] + first + t) % chunks)

    return pl.pallas_call(
        functools.partial(turn_sum_kernel, classes_here, rotations, count),
        grid_spec=pltpu.PrefetchScalarGridSpec(
            num_scalar_prefetch=1,
            grid=(count,),
            in_specs=[
                pl.BlockSpec((local_refs, n), lambda t, me_ref: (0, 0)),
                pl.BlockSpec((n, width), chunk_of),
                pl.BlockSpec((1, width), lambda t, me_ref: (0, 0)),
            ],
            out_specs=[
                pl.BlockSpec((classes_here, width + LANES), lambda t, me_ref: (0, 0))
                for _ in range(count)
            ],
            scratch_shapes=[
                pltpu.VMEM((local_refs, width), jnp.float32),
                pltpu.VMEM((classes_here, width + LANES), jnp.float32),
            ],
        ),
        out_shape=[
            jax.ShapeDtypeStruct((classes_here, width + LANES), jnp.float32) for _ in range(count)
        ],
        compiler_params=pltpu.CompilerParams(vmem_limit_bytes=60 * 1024 * 1024),
        cost_estimate=pl.CostEstimate(
            flops=2 * local_refs * n * width * count,
            bytes_accessed=2 * local_refs * n + 2 * n * width * count + 4 * classes_here * width * count,
            transcendentals=0,
        ),
    )(jnp.reshape(me, (1,)).astype(jnp.int32), by_turn, gathered, angle)

def ring_order(chips):
    if chips == 4:
        return [0, 1, 3, 2]
    order = []
    for row in range(chips // 2):
        order += [2 * row, 2 * row + 1] if row % 2 == 0 else [2 * row + 1, 2 * row]
    return order


def ring_gather(images, n_ref):
    chips = n_ref // 2
    block = images.shape[0]
    ring = ring_order(chips)
    place = {chip: i for i, chip in enumerate(ring)}

    def ahead(chip, hops):
        return ring[(place[chip] + hops) % chips]

    to_next = [(2 * c + k, 2 * ahead(c, 1) + k) for c in range(chips) for k in range(2)]
    to_prev = [(2 * c + k, 2 * ahead(c, -1) + k) for c in range(chips) for k in range(2)]
    to_partner = [(d, d ^ 1) for d in range(n_ref)]
    pieces = [(images, 0, 0, block)]
    from_prev = images
    from_next = images
    for hops in range(1, (chips + 1) // 2):
        from_prev = lax.ppermute(from_prev, "ref", to_next)
        from_next = lax.ppermute(from_next, "ref", to_prev)
        pieces += [(from_prev, -hops, 0, block), (from_next, hops, 0, block)]
    if chips % 2 == 0:
        half = block // 2
        top = lax.ppermute(from_prev[:half], "ref", to_next)
        bottom = lax.ppermute(from_next[half:], "ref", to_prev)
        pieces += [(top, chips // 2, 0, half), (bottom, chips // 2, half, block - half)]
    arrays = [piece[0] for piece in pieces]
    arrays += [lax.ppermute(piece[0], "ref", to_partner) for piece in pieces]
    table = []
    for device in range(n_ref):
        chip, core = device // 2, device % 2
        rows = []
        for side in (core, 1 - core):
            for _, hops, first, count in pieces:
                origin = 2 * ahead(chip, hops) + side
                rows += list(range(origin * block + first, origin * block + first + count))
        table.append(rows)
    return jnp.concatenate(arrays, axis=0), np.array(table, np.int32)


def per_device(chunks, n_ref, images, references, class_prior):
    local_refs, pixels = references.shape
    classes_here = class_prior.shape[0]
    rotations = local_refs // classes_here

    half_norm = 0.5 * jnp.einsum(
        "jp,jp->j", references, references, preferred_element_type=jnp.float32
    )
    offsets = (jnp.log(class_prior)[:, None] - half_norm.reshape(classes_here, rotations)).reshape(
        local_refs
    )
    gathered, table = ring_gather(images, n_ref)
    to_group = jnp.asarray(table)[lax.axis_index("ref")]
    from_group = jnp.asarray(np.argsort(table, axis=1).astype(np.int32))[lax.axis_index("ref")]
    products = lax.dot_general(
        gathered, references, (((1,), (1,)), ((), ())), preferred_element_type=jnp.float32
    )
    scores = products + offsets
    local_max = jnp.max(scores, axis=1)
    local_sum = jnp.sum(jnp.exp(scores - local_max[:, None]), axis=1)
    in_group_order = jnp.take(jnp.stack([local_max, local_sum]), from_group, axis=1)
    stats = lax.all_gather(in_group_order, "ref", axis=0)
    top_score = jnp.max(stats[:, 0], axis=0)
    denominator = jnp.sum(stats[:, 1] * jnp.exp(stats[:, 0] - top_score[None, :]), axis=0)
    norm = jnp.take(jnp.stack([top_score, denominator]), to_group, axis=1)
    top_score, denominator = norm[0], norm[1]
    weights = (jnp.exp(scores - top_score[:, None]) / denominator[:, None]).astype(jnp.bfloat16)

    n = weights.shape[0]
    by_turn = weights.reshape(n, classes_here, rotations).transpose(2, 1, 0).reshape(local_refs, n)
    me = lax.axis_index("img")
    received = []
    if chunks > 1:
        outgoing = turn_and_sum(by_turn, gathered, classes_here, rotations, chunks, me, 1, chunks - 1)
        received = [
            lax.ppermute(outgoing[step - 1], "img", [(src, (src + step) % chunks) for src in range(chunks)])
            for step in reversed(range(1, chunks))
        ]
    total = turn_and_sum(by_turn, gathered, classes_here, rotations, chunks, me, 0, 1)[0]
    for part in received:
        total = total + part
    width = pixels // chunks
    class_sums, class_weights = total[:, :width], total[:, width]
    return (class_sums, class_weights)

def solution(mesh):
    placed = (P(("img", "ref"), None), P("ref", None), P("ref"))
    return jax.shard_map(
        functools.partial(per_device, mesh.shape["img"], mesh.shape["ref"]),
        mesh=mesh,
        in_specs=placed,
        out_specs=(P("ref", "img"), P("ref")),
        check_vma=False,
    )
```

```python
import functools

import jax
import numpy as np
import jax.numpy as jnp
from jax import lax
from jax.experimental import pallas as pl
from jax.experimental.pallas import tpu as pltpu
from jax.sharding import PartitionSpec as P

ANG = 144
LANES = 128
GROUP_COLS = 1152


def turn_sum_kernel(classes_here, rotations, count, me_ref, by_turn_ref, images_ref, angle_ref, *rest):
    out_refs, products_ref, out_ref = rest[:count], rest[count], rest[count + 1]
    shift = ANG // rotations
    width = images_ref.shape[1]
    products_ref[...] = jnp.dot(
        by_turn_ref[...], images_ref[...], preferred_element_type=jnp.float32
    )
    rows = 8 if classes_here % 8 == 0 else classes_here
    cols = GROUP_COLS if width % GROUP_COLS == 0 else width
    for row0 in range(0, classes_here, rows):
        for col0 in range(0, width, cols):
            angle = angle_ref[:, col0 : col0 + cols]
            kept = products_ref[row0 : row0 + rows, col0 : col0 + cols]
            every = None
            for turn_index in range(1, rotations):
                start = turn_index * classes_here + row0
                part = products_ref[start : start + rows, col0 : col0 + cols]
                step = turn_index * shift
                ahead = pltpu.roll(part, cols - step, 1)
                kept = kept + jnp.where(angle < ANG - step, ahead, 0.0)
                every = ahead if every is None else every + ahead
            wrapped = every - (kept - products_ref[row0 : row0 + rows, col0 : col0 + cols])
            out_ref[row0 : row0 + rows, col0 : col0 + cols] = kept + pltpu.roll(wrapped, ANG, 1)
    mass = jnp.sum(by_turn_ref[...].astype(jnp.float32), axis=1, keepdims=True)
    class_mass = mass[0:classes_here]
    for turn_index in range(1, rotations):
        class_mass = class_mass + mass[turn_index * classes_here : (turn_index + 1) * classes_here]
    out_ref[:, width:] = jnp.broadcast_to(class_mass, (classes_here, LANES))
    step = pl.program_id(0)
    for index, target in enumerate(out_refs):

        @pl.when(step == index)
        def _():
            target[...] = out_ref[...]


def turn_and_sum(by_turn, gathered, classes_here, rotations, chunks, chunk_ids):
    local_refs, n = by_turn.shape
    pixels = gathered.shape[1]
    width = pixels // chunks
    count = chunk_ids.shape[0]
    angle = (jnp.arange(width, dtype=jnp.int32) % ANG).reshape(1, width)

    def chunk_of(t, ids_ref):
        return (0, ids_ref[t])

    return pl.pallas_call(
        functools.partial(turn_sum_kernel, classes_here, rotations, count),
        grid_spec=pltpu.PrefetchScalarGridSpec(
            num_scalar_prefetch=1,
            grid=(count,),
            in_specs=[
                pl.BlockSpec((local_refs, n), lambda t, me_ref: (0, 0)),
                pl.BlockSpec((n, width), chunk_of),
                pl.BlockSpec((1, width), lambda t, me_ref: (0, 0)),
            ],
            out_specs=[
                pl.BlockSpec((classes_here, width + LANES), lambda t, me_ref: (0, 0))
                for _ in range(count)
            ],
            scratch_shapes=[
                pltpu.VMEM((local_refs, width), jnp.float32),
                pltpu.VMEM((classes_here, width + LANES), jnp.float32),
            ],
        ),
        out_shape=[
            jax.ShapeDtypeStruct((classes_here, width + LANES), jnp.float32) for _ in range(count)
        ],
        compiler_params=pltpu.CompilerParams(vmem_limit_bytes=60 * 1024 * 1024),
        cost_estimate=pl.CostEstimate(
            flops=2 * local_refs * n * width * count,
            bytes_accessed=2 * local_refs * n + 2 * n * width * count + 4 * classes_here * width * count,
            transcendentals=0,
        ),
    )(chunk_ids.astype(jnp.int32), by_turn, gathered, angle)

def ring_order(chips):
    if chips == 4:
        return [0, 1, 3, 2]
    order = []
    for row in range(chips // 2):
        order += [2 * row, 2 * row + 1] if row % 2 == 0 else [2 * row + 1, 2 * row]
    return order


def ring_gather(images, n_ref):
    chips = n_ref // 2
    block = images.shape[0]
    ring = ring_order(chips)
    place = {chip: i for i, chip in enumerate(ring)}

    def ahead(chip, hops):
        return ring[(place[chip] + hops) % chips]

    to_next = [(2 * c + k, 2 * ahead(c, 1) + k) for c in range(chips) for k in range(2)]
    to_prev = [(2 * c + k, 2 * ahead(c, -1) + k) for c in range(chips) for k in range(2)]
    to_partner = [(d, d ^ 1) for d in range(n_ref)]
    pieces = [(images, 0, 0, block)]
    from_prev = images
    from_next = images
    for hops in range(1, (chips + 1) // 2):
        from_prev = lax.ppermute(from_prev, "ref", to_next)
        from_next = lax.ppermute(from_next, "ref", to_prev)
        pieces += [(from_prev, -hops, 0, block), (from_next, hops, 0, block)]
    if chips % 2 == 0:
        half = block // 2
        top = lax.ppermute(from_prev[:half], "ref", to_next)
        bottom = lax.ppermute(from_next[half:], "ref", to_prev)
        pieces += [(top, chips // 2, 0, half), (bottom, chips // 2, half, block - half)]
    arrays = [piece[0] for piece in pieces]
    arrays += [lax.ppermute(piece[0], "ref", to_partner) for piece in pieces]
    table = []
    for device in range(n_ref):
        chip, core = device // 2, device % 2
        rows = []
        for side in (core, 1 - core):
            for _, hops, first, count in pieces:
                origin = 2 * ahead(chip, hops) + side
                rows += list(range(origin * block + first, origin * block + first + count))
        table.append(rows)
    return jnp.concatenate(arrays, axis=0), np.array(table, np.int32)


def per_device(chunks, n_ref, images, references, class_prior):
    local_refs, pixels = references.shape
    classes_here = class_prior.shape[0]
    rotations = local_refs // classes_here

    half_norm = 0.5 * jnp.einsum(
        "jp,jp->j", references, references, preferred_element_type=jnp.float32
    )
    offsets = (jnp.log(class_prior)[:, None] - half_norm.reshape(classes_here, rotations)).reshape(
        local_refs
    )
    gathered, table = ring_gather(images, n_ref)
    to_group = jnp.asarray(table)[lax.axis_index("ref")]
    from_group = jnp.asarray(np.argsort(table, axis=1).astype(np.int32))[lax.axis_index("ref")]
    products = lax.dot_general(
        gathered, references, (((1,), (1,)), ((), ())), preferred_element_type=jnp.float32
    )
    scores = products + offsets
    local_max = jnp.max(scores, axis=1)
    local_sum = jnp.sum(jnp.exp(scores - local_max[:, None]), axis=1)
    in_group_order = jnp.take(jnp.stack([local_max, local_sum]), from_group, axis=1)
    stats = lax.all_gather(in_group_order, "ref", axis=0)
    top_score = jnp.max(stats[:, 0], axis=0)
    denominator = jnp.sum(stats[:, 1] * jnp.exp(stats[:, 0] - top_score[None, :]), axis=0)
    norm = jnp.take(jnp.stack([top_score, denominator]), to_group, axis=1)
    top_score, denominator = norm[0], norm[1]
    weights = (jnp.exp(scores - top_score[:, None]) / denominator[:, None]).astype(jnp.bfloat16)

    n = weights.shape[0]
    by_turn = weights.reshape(n, classes_here, rotations).transpose(2, 1, 0).reshape(local_refs, n)
    me = lax.axis_index("img")
    received = []
    if chunks > 1:
        order = [chunks // 2] + [step for step in range(1, chunks) if step != chunks // 2]
        for steps in (order[:1], order[1:]):
            if not steps:
                continue
            ids = (me + jnp.array(steps, jnp.int32)) % chunks
            parts = turn_and_sum(by_turn, gathered, classes_here, rotations, chunks, ids)
            for step, part in zip(steps, parts):
                perm = [(src, (src + step) % chunks) for src in range(chunks)]
                received.append(lax.ppermute(part, "img", perm))
    total = turn_and_sum(by_turn, gathered, classes_here, rotations, chunks, jnp.reshape(me, (1,)))[0]
    for part in received:
        total = total + part
    width = pixels // chunks
    class_sums, class_weights = total[:, :width], total[:, width]
    return (class_sums, class_weights)

def solution(mesh):
    placed = (P(("img", "ref"), None), P("ref", None), P("ref"))
    return jax.shard_map(
        functools.partial(per_device, mesh.shape["img"], mesh.shape["ref"]),
        mesh=mesh,
        in_specs=placed,
        out_specs=(P("ref", "img"), P("ref")),
        check_vma=False,
    )
```

```python
import functools

import jax
import numpy as np
import jax.numpy as jnp
from jax import lax
from jax.experimental import pallas as pl
from jax.experimental.pallas import tpu as pltpu
from jax.sharding import PartitionSpec as P

ANG = 144
LANES = 128
GROUP_COLS = 1152


def turn_sum_kernel(classes_here, rotations, count, me_ref, by_turn_ref, images_ref, angle_ref, *rest):
    out_refs, products_ref, out_ref = rest[:count], rest[count], rest[count + 1]
    shift = ANG // rotations
    width = images_ref.shape[1]
    products_ref[...] = jnp.dot(
        by_turn_ref[...], images_ref[...], preferred_element_type=jnp.float32
    )
    rows = 8 if classes_here % 8 == 0 else classes_here
    cols = GROUP_COLS if width % GROUP_COLS == 0 else width
    for row0 in range(0, classes_here, rows):
        for col0 in range(0, width, cols):
            angle = angle_ref[:, col0 : col0 + cols]
            kept = products_ref[row0 : row0 + rows, col0 : col0 + cols]
            every = None
            for turn_index in range(1, rotations):
                start = turn_index * classes_here + row0
                part = products_ref[start : start + rows, col0 : col0 + cols]
                step = turn_index * shift
                ahead = pltpu.roll(part, cols - step, 1)
                kept = kept + jnp.where(angle < ANG - step, ahead, 0.0)
                every = ahead if every is None else every + ahead
            wrapped = every - (kept - products_ref[row0 : row0 + rows, col0 : col0 + cols])
            out_ref[row0 : row0 + rows, col0 : col0 + cols] = kept + pltpu.roll(wrapped, ANG, 1)
    mass = jnp.sum(by_turn_ref[...].astype(jnp.float32), axis=1, keepdims=True)
    class_mass = mass[0:classes_here]
    for turn_index in range(1, rotations):
        class_mass = class_mass + mass[turn_index * classes_here : (turn_index + 1) * classes_here]
    out_ref[:, width:] = jnp.broadcast_to(class_mass, (classes_here, LANES))
    step = pl.program_id(0)
    for index, target in enumerate(out_refs):

        @pl.when(step == index)
        def _():
            target[...] = out_ref[...]


def turn_and_sum(by_turn, gathered, classes_here, rotations, chunks, chunk_ids):
    local_refs, n = by_turn.shape
    pixels = gathered.shape[1]
    width = pixels // chunks
    count = chunk_ids.shape[0]
    angle = (jnp.arange(width, dtype=jnp.int32) % ANG).reshape(1, width)

    def chunk_of(t, ids_ref):
        return (0, ids_ref[t])

    return pl.pallas_call(
        functools.partial(turn_sum_kernel, classes_here, rotations, count),
        grid_spec=pltpu.PrefetchScalarGridSpec(
            num_scalar_prefetch=1,
            grid=(count,),
            in_specs=[
                pl.BlockSpec((local_refs, n), lambda t, me_ref: (0, 0)),
                pl.BlockSpec((n, width), chunk_of),
                pl.BlockSpec((1, width), lambda t, me_ref: (0, 0)),
            ],
            out_specs=[
                pl.BlockSpec((classes_here, width + LANES), lambda t, me_ref: (0, 0))
                for _ in range(count)
            ],
            scratch_shapes=[
                pltpu.VMEM((local_refs, width), jnp.float32),
                pltpu.VMEM((classes_here, width + LANES), jnp.float32),
            ],
        ),
        out_shape=[
            jax.ShapeDtypeStruct((classes_here, width + LANES), jnp.float32) for _ in range(count)
        ],
        compiler_params=pltpu.CompilerParams(vmem_limit_bytes=60 * 1024 * 1024),
        cost_estimate=pl.CostEstimate(
            flops=2 * local_refs * n * width * count,
            bytes_accessed=2 * local_refs * n + 2 * n * width * count + 4 * classes_here * width * count,
            transcendentals=0,
        ),
    )(chunk_ids.astype(jnp.int32), by_turn, gathered, angle)

def ring_order(chips):
    if chips == 4:
        return [0, 1, 3, 2]
    order = []
    for row in range(chips // 2):
        order += [2 * row, 2 * row + 1] if row % 2 == 0 else [2 * row + 1, 2 * row]
    return order


def ring_gather(images, n_ref):
    chips = n_ref // 2
    block = images.shape[0]
    ring = ring_order(chips)
    place = {chip: i for i, chip in enumerate(ring)}

    def ahead(chip, hops):
        return ring[(place[chip] + hops) % chips]

    to_next = [(2 * c + k, 2 * ahead(c, 1) + k) for c in range(chips) for k in range(2)]
    to_prev = [(2 * c + k, 2 * ahead(c, -1) + k) for c in range(chips) for k in range(2)]
    to_partner = [(d, d ^ 1) for d in range(n_ref)]
    pieces = [(images, 0, 0, block)]
    from_prev = images
    from_next = images
    for hops in range(1, (chips + 1) // 2):
        from_prev = lax.ppermute(from_prev, "ref", to_next)
        from_next = lax.ppermute(from_next, "ref", to_prev)
        pieces += [(from_prev, -hops, 0, block), (from_next, hops, 0, block)]
    if chips % 2 == 0:
        half = block // 2
        top = lax.ppermute(from_prev[:half], "ref", to_next)
        bottom = lax.ppermute(from_next[half:], "ref", to_prev)
        pieces += [(top, chips // 2, 0, half), (bottom, chips // 2, half, block - half)]
    arrays = [piece[0] for piece in pieces]
    arrays += [lax.ppermute(piece[0], "ref", to_partner) for piece in pieces]
    table = []
    for device in range(n_ref):
        chip, core = device // 2, device % 2
        rows = []
        for side in (core, 1 - core):
            for _, hops, first, count in pieces:
                origin = 2 * ahead(chip, hops) + side
                rows += list(range(origin * block + first, origin * block + first + count))
        table.append(rows)
    return jnp.concatenate(arrays, axis=0), np.array(table, np.int32)


def per_device(chunks, n_ref, images, references, class_prior):
    local_refs, pixels = references.shape
    classes_here = class_prior.shape[0]
    rotations = local_refs // classes_here

    half_norm = 0.5 * jnp.einsum(
        "jp,jp->j", references, references, preferred_element_type=jnp.float32
    )
    offsets = (jnp.log(class_prior)[:, None] - half_norm.reshape(classes_here, rotations)).reshape(
        local_refs
    )
    gathered, table = ring_gather(images, n_ref)
    to_group = jnp.asarray(table)[lax.axis_index("ref")]
    from_group = jnp.asarray(np.argsort(table, axis=1).astype(np.int32))[lax.axis_index("ref")]
    products = lax.dot_general(
        gathered, references, (((1,), (1,)), ((), ())), preferred_element_type=jnp.float32
    )
    scores = products + offsets
    local_max = jnp.max(scores, axis=1)
    local_sum = jnp.sum(jnp.exp(scores - local_max[:, None]), axis=1)
    in_group_order = jnp.take(jnp.stack([local_max, local_sum]), from_group, axis=1)
    stats = lax.all_gather(in_group_order, "ref", axis=0)
    top_score = jnp.max(stats[:, 0], axis=0)
    denominator = jnp.sum(stats[:, 1] * jnp.exp(stats[:, 0] - top_score[None, :]), axis=0)
    norm = jnp.take(jnp.stack([top_score, denominator]), to_group, axis=1)
    top_score, denominator = norm[0], norm[1]
    weights = (jnp.exp(scores - top_score[:, None]) / denominator[:, None]).astype(jnp.bfloat16)

    n = weights.shape[0]
    by_turn = weights.reshape(n, classes_here, rotations).transpose(2, 1, 0).reshape(local_refs, n)
    me = lax.axis_index("img")
    received = []
    if chunks > 1:
        order = [chunks // 2] + [step for step in range(1, chunks) if step != chunks // 2]
        for steps in [[step] for step in order]:
            if not steps:
                continue
            ids = (me + jnp.array(steps, jnp.int32)) % chunks
            parts = turn_and_sum(by_turn, gathered, classes_here, rotations, chunks, ids)
            for step, part in zip(steps, parts):
                perm = [(src, (src + step) % chunks) for src in range(chunks)]
                received.append(lax.ppermute(part, "img", perm))
    total = turn_and_sum(by_turn, gathered, classes_here, rotations, chunks, jnp.reshape(me, (1,)))[0]
    for part in received:
        total = total + part
    width = pixels // chunks
    class_sums, class_weights = total[:, :width], total[:, width]
    return (class_sums, class_weights)

def solution(mesh):
    placed = (P(("img", "ref"), None), P("ref", None), P("ref"))
    return jax.shard_map(
        functools.partial(per_device, mesh.shape["img"], mesh.shape["ref"]),
        mesh=mesh,
        in_specs=placed,
        out_specs=(P("ref", "img"), P("ref")),
        check_vma=False,
    )
```
